512 devices in a mesh: dp: 64 (over z, y), seq: 8 (over x, core).
Axes of the slice: x: 4, y: 8, z: 8, core: 2. Of those that a mesh axis runs over, the one named last changes fastest.
Arguments:
- checkpoint: bfloat16 [65536, 8192], P(('dp', 'seq')), may hold values from -6 to 6
- norm_gain: float32 [8192], replicated, may hold values from 0.1 to 1.9
- key_cotangent: bfloat16 [65536, 1024], P(('dp', 'seq')), may hold values from -6 to 6
- positions: int32 [65536], P(('dp', 'seq')), may hold values from 0 to 4095, as said below
- kept_cols: int32 [128, 6], replicated, may hold values from 0 to 15, as said below
- kept_count: int32 [128], replicated, may hold values from 2 to 6
- key_blocks: bfloat16 [128, 6, 4096], P('dp'), may hold values from -0.375 to 0.375
Outputs:
- input_grad: bfloat16 [65536, 8192], P(('dp', 'seq'))
- block_grad: float32 [128, 6, 4096], P('dp', None, 'seq')
The draws below stay inside these ranges and needn't reach their ends.
Inputs may be any that keep to these rules, and one draw needn't show every extreme that they name: `kept_cols`: the 6 entries of a row are different block columns; only the first kept_count entries of a row name kept blocks, the others are unused slots. Inside a document the positions rise by one from token to token.
All inputs are finite; a program needn't handle non-finite values.
Results may differ from the reference program's by a relative error of at most 0.0049.
Values may be sent and summed in bfloat16 or wider, within the bound.
No kernel may reach another device: no remote copies, remote signals or barrier semaphores. Data moves between devices by JAX's collectives and lax.ppermute only.
A program may use at most 128 MiB of HBM per device.

```python
import jax
import jax.numpy as jnp
from jax import lax

D = 8192
KVW = 1024
HEAD_DIM = 128
BLK = 64
MOSTR = 6
SEQ_LEN = 1024
TOKENS = 65536
ROW_BLOCKS = 128


def draw_positions(key, part):
    key = jax.random.fold_in(key, 101)
    first_key, second_key = jax.random.split(key)
    index = jnp.arange(TOKENS, dtype=jnp.int32)
    inside = index % SEQ_LEN
    seq_ids = index // SEQ_LEN
    begins = (jax.random.randint(first_key, (TOKENS,), 0, 400) == 0) & (seq_ids != 0) | (inside == 0)
    last = lax.cummax(jnp.where(begins, index, 0), axis=0)
    seqs = TOKENS // SEQ_LEN
    offset = jax.random.randint(second_key, (seqs,), 0, 4096 - SEQ_LEN + 1)
    seq_index = jnp.arange(seqs, dtype=jnp.int32)
    offset = jnp.where(seq_index == 0, 4096 - SEQ_LEN, offset)
    offset = jnp.where(seq_index == 1, 0, offset)
    carried = jnp.repeat(offset, SEQ_LEN)
    first_doc = last % SEQ_LEN == 0
    return (index - last + jnp.where(first_doc, carried, 0)).astype(jnp.int32)


def draw_kept_cols(key, part):
    key = jax.random.fold_in(key, 202)
    rows = D // BLK
    cols = KVW // BLK
    scores = jax.random.randint(key, (rows, cols), 0, 1 << 20) * cols + jnp.arange(cols, dtype=jnp.int32)[None, :]
    order = jnp.argsort(scores, axis=1)
    return order[:, :MOSTR].astype(jnp.int32)


def draw_kept_count(key, part):
    key = jax.random.fold_in(key, 303)
    rows = D // BLK
    first_key, second_key = jax.random.split(key)
    counts = jax.random.randint(first_key, (rows,), 2, MOSTR + 1)
    full = jax.random.randint(second_key, (), 0, rows)
    index = jnp.arange(rows, dtype=jnp.int32)
    counts = jnp.where(index == full, MOSTR, counts)
    counts = jnp.where(index == (full + rows // 2) % rows, 2, counts)
    return counts.astype(jnp.int32)


def levels(rng, dims, cuts, low, top_value):
    def one(dim, shards_of):
        heights = jax.random.uniform(jax.random.fold_in(jax.random.fold_in(rng, 6), dim), (shards_of,), jnp.float32, low / len(cuts), top_value / len(cuts))
        return jnp.repeat(jnp.exp(heights), dims[dim] // shards_of).reshape((-1,) + (1,) * (len(dims) - dim - 1))

    factor_of = one(*cuts[0])
    for cut in cuts[1:]:
        factor_of = factor_of * one(*cut)
    return factor_of


def bell_draw(own_key, extent, scale, limit, cuts=(), kind=jnp.bfloat16):
    entries = scale * jax.random.normal(own_key, extent, jnp.float32)
    if cuts:
        entries = entries * levels(own_key, extent, cuts, -0.22, 0.18)
    return jnp.clip(entries, -limit, limit).astype(kind)


def setup_inputs(seed: int = 0) -> dict:
    keys = jax.random.split(jax.random.key(seed), 8)
    checkpoint = bell_draw(keys[0], (TOKENS, D), 1.0, 6.0, ((0, 512),))
    norm_gain = jnp.clip(1.0 + 0.18 * jax.random.normal(keys[1], (D,), jnp.float32), 0.1, 1.9)
    key_cotangent = bell_draw(keys[2], (TOKENS, KVW), 1.0, 6.0, ((0, 512),))
    positions = draw_positions(jax.random.fold_in(keys[7], 71), 0)
    kept_cols = draw_kept_cols(jax.random.fold_in(keys[7], 71), 0)
    kept_count = draw_kept_count(jax.random.fold_in(keys[7], 71), 0)
    key_blocks = bell_draw(keys[6], (ROW_BLOCKS, MOSTR, BLK * BLK), (4 * BLK) ** -0.5, 0.375, ((0, 64),))
    return dict(checkpoint=checkpoint, norm_gain=norm_gain, key_cotangent=key_cotangent, positions=positions, kept_cols=kept_cols, kept_count=kept_count, key_blocks=key_blocks)


def rope_back(grad, positions):
    heads = KVW // HEAD_DIM
    half = HEAD_DIM // 2
    values = grad.astype(jnp.float32).reshape(-1, heads, 2, half)
    freqs = 10000.0 ** (-2.0 * jnp.arange(half).astype(jnp.float32) / HEAD_DIM)
    angle = positions.astype(jnp.float32)[:, None] * freqs[None, :]
    cosine = jnp.cos(angle)[:, None, :]
    sine = jnp.sin(angle)[:, None, :]
    first = values[:, :, 0] * cosine + values[:, :, 1] * sine
    second = values[:, :, 1] * cosine - values[:, :, 0] * sine
    return jnp.stack([first, second], axis=2).reshape(-1, KVW).astype(jnp.bfloat16)

def densify(blocks, cols, count, rows):
    count_rows = blocks.shape[0]
    col_blocks = KVW // BLK
    live = jnp.arange(MOSTR)[None, :] < count[:, None]
    onehot = ((cols[:, :, None] == jnp.arange(col_blocks)[None, None, :]) & live[:, :, None]).astype(jnp.float32)
    shaped = blocks.astype(jnp.float32).reshape(count_rows, MOSTR, rows, BLK)
    dense = jnp.einsum('nkc,nkij->nicj', onehot, shaped)
    return dense.reshape(count_rows * rows, KVW).astype(jnp.bfloat16)

def reference(checkpoint, norm_gain, key_cotangent, positions, kept_cols, kept_count, key_blocks):
    weight = densify(key_blocks, kept_cols, kept_count, BLK)
    seqs = TOKENS // SEQ_LEN

    def one_sequence(total, pieces):
        rows, cots, pos = pieces
        xf = rows.astype(jnp.float32)
        inv_rms = lax.rsqrt(lax.optimization_barrier(jnp.mean(xf * xf, axis=1, keepdims=True)) + 1e-05)
        normed = (xf * inv_rms * norm_gain).astype(jnp.bfloat16)
        grad_pre = rope_back(cots, pos)
        normed_grad = jnp.dot(grad_pre, weight.T, preferred_element_type=jnp.float32)
        scaled = norm_gain * normed_grad
        grads = inv_rms * scaled - inv_rms ** 3 * xf * lax.optimization_barrier(jnp.mean(scaled * xf, axis=1, keepdims=True))
        total = total + jnp.dot(normed.T, grad_pre, preferred_element_type=jnp.float32)
        return (total, grads.astype(jnp.bfloat16))
    init = jnp.zeros((D, KVW), jnp.float32)
    sums, grads = lax.scan(one_sequence, init, (checkpoint.reshape(seqs, SEQ_LEN, D), key_cotangent.reshape(seqs, SEQ_LEN, KVW), positions.reshape(seqs, SEQ_LEN)))
    input_grad = grads.reshape(TOKENS, D)
    row_blocks = D // BLK
    col_blocks = KVW // BLK
    shaped = sums.reshape(row_blocks, BLK, col_blocks, BLK).transpose(0, 2, 1, 3).reshape(row_blocks, col_blocks, BLK * BLK)
    picked = jnp.take_along_axis(shaped, kept_cols[:, :, None], axis=1)
    live = jnp.arange(MOSTR)[None, :] < kept_count[:, None]
    block_grad = jnp.where(live[:, :, None], picked / jnp.sqrt(jnp.float32(TOKENS)), jnp.float32(0.0))
    return (input_grad, block_grad)
```

```python
import math

import jax
import jax.numpy as jnp
import numpy as np
from jax import lax
from jax.experimental import pallas as pl
from jax.experimental.pallas import tpu as pltpu
from jax.sharding import Mesh
from jax.sharding import PartitionSpec as P

D = 8192
KVW = 1024
HEAD_DIM = 128
BLK = 64
MOSTR = 6
SEQ_LEN = 1024
ROWS_PER_STEP = 8


def rope_back(grad, positions):
    heads = KVW // HEAD_DIM
    half = HEAD_DIM // 2
    values = grad.astype(jnp.float32).reshape(-1, heads, 2, half)
    freqs = 10000.0 ** (-2.0 * jnp.arange(half).astype(jnp.float32) / HEAD_DIM)
    angle = positions.astype(jnp.float32)[:, None] * freqs[None, :]
    cosine = jnp.cos(angle)[:, None, :]
    sine = jnp.sin(angle)[:, None, :]
    first = values[:, :, 0] * cosine + values[:, :, 1] * sine
    second = values[:, :, 1] * cosine - values[:, :, 0] * sine
    return jnp.stack([first, second], axis=2).reshape(-1, KVW).astype(jnp.bfloat16)


def _normed_grad_kernel(cols_ref, cnt_ref, gp_ref, bt_ref, out_ref, w_ref):
    step = pl.program_id(0)
    w_ref[...] = jnp.zeros(w_ref.shape, w_ref.dtype)
    for rr in range(ROWS_PER_STEP):
        row = step * ROWS_PER_STEP + rr
        live = cnt_ref[row]
        for k in range(MOSTR):
            col = cols_ref[row * MOSTR + k]

            @pl.when(k < live)
            def _():
                start = pl.multiple_of(col * BLK, BLK)
                w_ref[pl.ds(start, BLK), rr * BLK:(rr + 1) * BLK] = bt_ref[rr, k].astype(jnp.float32)

    out_ref[...] = jnp.dot(
        gp_ref[...], w_ref[...].astype(jnp.bfloat16), preferred_element_type=jnp.float32
    )


def normed_grad_of(grad_pre, blocks_t, cols, counts):
    tok = grad_pre.shape[0]
    row_blocks = blocks_t.shape[0]
    width = ROWS_PER_STEP * BLK
    spec = pltpu.PrefetchScalarGridSpec(
        num_scalar_prefetch=2,
        grid=(row_blocks // ROWS_PER_STEP,),
        in_specs=[
            pl.BlockSpec((tok, KVW), lambda g, c, n: (0, 0)),
            pl.BlockSpec((ROWS_PER_STEP, MOSTR, BLK, BLK), lambda g, c, n: (g, 0, 0, 0)),
        ],
        out_specs=pl.BlockSpec((tok, width), lambda g, c, n: (0, g)),
        scratch_shapes=[pltpu.VMEM((KVW, width), jnp.float32)],
    )
    return pl.pallas_call(
        _normed_grad_kernel,
        grid_spec=spec,
        out_shape=jax.ShapeDtypeStruct((tok, row_blocks * BLK), jnp.float32),
    )(cols.reshape(-1), counts, grad_pre, blocks_t)


def shards(checkpoint, norm_gain, key_cotangent, positions, kept_cols, kept_count, key_blocks):
    tok_rows = checkpoint.shape[0]
    groups = lax.axis_size("x") * lax.axis_size("c")
    dp_size = lax.axis_size("z") * lax.axis_size("y")
    part_rows = BLK // groups
    row_blocks = D // BLK
    col_blocks = KVW // BLK
    xf = checkpoint.astype(jnp.float32)
    inv_rms = lax.rsqrt(jnp.mean(xf * xf, axis=1, keepdims=True) + 1e-05)
    normed = (xf * inv_rms * norm_gain).astype(jnp.bfloat16)
    grad_pre = rope_back(key_cotangent, positions)

    local_t = key_blocks.reshape(key_blocks.shape[0], MOSTR, BLK, BLK).transpose(0, 1, 3, 2)
    piece = lax.all_gather(local_t, "y", axis=0, tiled=True)
    piece = lax.all_gather(piece, "z", axis=0, tiled=True)

    grad_all = lax.all_gather(grad_pre, ("x", "c"), axis=0, tiled=True)
    split_normed = (
        normed.reshape(tok_rows, row_blocks, groups, part_rows)
        .transpose(0, 2, 1, 3)
        .reshape(tok_rows, groups, row_blocks * part_rows)
    )
    received = lax.all_to_all(split_normed, ("x", "c"), split_axis=1, concat_axis=0, tiled=True)
    normed_rows = received.reshape(groups * tok_rows, row_blocks, part_rows)
    divisor = math.sqrt(SEQ_LEN * dp_size)
    count = row_blocks
    slab = normed_rows.reshape(groups * tok_rows, count * part_rows)
    product = lax.dot_general(
        slab, grad_all, (((0,), (0,)), ((), ())), preferred_element_type=jnp.float32
    )
    shaped = (
        product.reshape(count, part_rows, col_blocks, BLK)
        .transpose(0, 2, 1, 3)
        .reshape(count, col_blocks, part_rows * BLK)
    )
    picked = jnp.take_along_axis(shaped, kept_cols[:, :, None], axis=1)
    live = lax.broadcasted_iota(jnp.int32, (count, MOSTR), 1) < kept_count[:, None]
    partial = jnp.where(live[:, :, None], picked / divisor, jnp.float32(0.0))
    block_grad = lax.psum_scatter(partial, "z", scatter_dimension=0, tiled=True)
    block_grad = lax.psum_scatter(block_grad, "y", scatter_dimension=0, tiled=True)

    normed_grad = normed_grad_of(grad_pre, piece, kept_cols, kept_count)
    scaled = norm_gain * normed_grad
    grads = inv_rms * scaled - inv_rms**3 * xf * jnp.mean(scaled * xf, axis=1, keepdims=True)
    return (grads.astype(jnp.bfloat16), block_grad)


def _split_mesh(mesh):
    devs = mesh.devices
    dp, seq = devs.shape
    ys = len({d.coords[1] for d in devs[:, 0]}) if hasattr(devs[0, 0], "coords") else 1
    cores = 2 if seq % 2 == 0 else 1
    return Mesh(devs.reshape(dp // ys, ys, seq // cores, cores), ("z", "y", "x", "c"))


def solution(mesh):
    fine = _split_mesh(mesh)
    rows = ("z", "y", "x", "c")
    placed = (
        P(rows, None),
        P(),
        P(rows, None),
        P(rows),
        P(),
        P(),
        P(("z", "y"), None, None),
    )
    return jax.shard_map(
        shards,
        mesh=fine,
        in_specs=placed,
        out_specs=(P(rows, None), P(("z", "y"), None, ("x", "c"))),
        check_vma=False,
    )
```

```python
import math

import jax
import jax.numpy as jnp
import numpy as np
from jax import lax
from jax.experimental import pallas as pl
from jax.experimental.pallas import tpu as pltpu
from jax.sharding import Mesh
from jax.sharding import PartitionSpec as P

D = 8192
KVW = 1024
HEAD_DIM = 128
BLK = 64
MOSTR = 6
SEQ_LEN = 1024
ROWS_PER_STEP = 8


def rope_back(grad, positions):
    heads = KVW // HEAD_DIM
    half = HEAD_DIM // 2
    values = grad.astype(jnp.float32).reshape(-1, heads, 2, half)
    freqs = 10000.0 ** (-2.0 * jnp.arange(half).astype(jnp.float32) / HEAD_DIM)
    angle = positions.astype(jnp.float32)[:, None] * freqs[None, :]
    cosine = jnp.cos(angle)[:, None, :]
    sine = jnp.sin(angle)[:, None, :]
    first = values[:, :, 0] * cosine + values[:, :, 1] * sine
    second = values[:, :, 1] * cosine - values[:, :, 0] * sine
    return jnp.stack([first, second], axis=2).reshape(-1, KVW).astype(jnp.bfloat16)


def _normed_grad_kernel(cols_ref, cnt_ref, gp_ref, bt_ref, out_ref, w_ref):
    step = pl.program_id(0)

    @pl.when(step == 0)
    def _():
        w_ref[...] = jnp.zeros(w_ref.shape, w_ref.dtype)

    def place(fill):
        for rr in range(ROWS_PER_STEP):
            row = step * ROWS_PER_STEP + rr
            live = cnt_ref[row]
            for k in range(MOSTR):
                col = cols_ref[row * MOSTR + k]

                @pl.when(k < live)
                def _():
                    start = pl.multiple_of(col * BLK, BLK)
                    half = (k % 2) * BLK
                    if fill:
                        value = bt_ref[rr, k // 2, :, half:half + BLK]
                    else:
                        value = jnp.zeros((BLK, BLK), w_ref.dtype)
                    w_ref[pl.ds(start, BLK), rr * BLK:(rr + 1) * BLK] = value

    place(True)
    out_ref[...] = jnp.dot(gp_ref[...], w_ref[...], preferred_element_type=jnp.float32)
    place(False)


def normed_grad_of(grad_pre, blocks_t, cols, counts):
    tok = grad_pre.shape[0]
    row_blocks = blocks_t.shape[0]
    width = ROWS_PER_STEP * BLK
    spec = pltpu.PrefetchScalarGridSpec(
        num_scalar_prefetch=2,
        grid=(row_blocks // ROWS_PER_STEP,),
        in_specs=[
            pl.BlockSpec((tok, KVW), lambda g, c, n: (0, 0)),
            pl.BlockSpec((ROWS_PER_STEP, MOSTR // 2, BLK, 2 * BLK), lambda g, c, n: (g, 0, 0, 0)),
        ],
        out_specs=pl.BlockSpec((tok, width), lambda g, c, n: (0, g)),
        scratch_shapes=[pltpu.VMEM((KVW, width), jnp.bfloat16)],
    )
    return pl.pallas_call(
        _normed_grad_kernel,
        grid_spec=spec,
        out_shape=jax.ShapeDtypeStruct((tok, row_blocks * BLK), jnp.float32),
        compiler_params=pltpu.CompilerParams(dimension_semantics=("arbitrary",)),
    )(cols.reshape(-1), counts, grad_pre, blocks_t)


def shards(checkpoint, norm_gain, key_cotangent, positions, kept_cols, kept_count, key_blocks):
    tok_rows = checkpoint.shape[0]
    groups = lax.axis_size("x") * lax.axis_size("c")
    dp_size = lax.axis_size("z") * lax.axis_size("y")
    part_rows = BLK // groups
    row_blocks = D // BLK
    col_blocks = KVW // BLK
    xf = checkpoint.astype(jnp.float32)
    inv_rms = lax.rsqrt(jnp.mean(xf * xf, axis=1, keepdims=True) + 1e-05)
    normed = (xf * inv_rms * norm_gain).astype(jnp.bfloat16)
    grad_pre = rope_back(key_cotangent, positions)

    local_t = (
        key_blocks.reshape(key_blocks.shape[0], MOSTR // 2, 2, BLK, BLK)
        .transpose(0, 1, 4, 2, 3)
        .reshape(key_blocks.shape[0], MOSTR // 2, BLK, 2 * BLK)
    )
    piece = lax.all_gather(local_t, ("z", "y"), axis=0, tiled=True)

    split_normed = (
        normed.reshape(tok_rows, row_blocks, groups, part_rows)
        .transpose(0, 2, 1, 3)
        .reshape(tok_rows, groups, row_blocks * part_rows)
    )
    sent = jnp.concatenate(
        [split_normed, jnp.broadcast_to(grad_pre[:, None, :], (tok_rows, groups, KVW))], axis=2
    )
    received = lax.all_to_all(sent, ("x", "c"), split_axis=1, concat_axis=0, tiled=True)
    received = received.reshape(groups * tok_rows, row_blocks * part_rows + KVW)
    grad_all = received[:, row_blocks * part_rows:]
    normed_rows = received[:, : row_blocks * part_rows].reshape(groups * tok_rows, row_blocks, part_rows)
    divisor = math.sqrt(SEQ_LEN * dp_size)
    count = row_blocks
    slab = normed_rows.reshape(groups * tok_rows, count * part_rows)
    product = lax.dot_general(
        slab, grad_all, (((0,), (0,)), ((), ())), preferred_element_type=jnp.float32
    )
    shaped = (
        product.reshape(count, part_rows, col_blocks, BLK)
        .transpose(0, 2, 1, 3)
        .reshape(count, col_blocks, part_rows * BLK)
    )
    picked = jnp.take_along_axis(shaped, kept_cols[:, :, None], axis=1)
    live = lax.broadcasted_iota(jnp.int32, (count, MOSTR), 1) < kept_count[:, None]
    partial = jnp.where(live[:, :, None], picked / divisor, jnp.float32(0.0))
    partial, piece = lax.optimization_barrier((partial, piece))
    block_grad = lax.psum_scatter(partial, "z", scatter_dimension=0, tiled=True)
    block_grad = lax.psum_scatter(block_grad, "y", scatter_dimension=0, tiled=True)

    normed_grad = normed_grad_of(grad_pre, piece, kept_cols, kept_count)
    scaled = norm_gain * normed_grad
    grads = inv_rms * scaled - inv_rms**3 * xf * jnp.mean(scaled * xf, axis=1, keepdims=True)
    return (grads.astype(jnp.bfloat16), block_grad)


def _split_mesh(mesh):
    devs = mesh.devices
    dp, seq = devs.shape
    ys = len({d.coords[1] for d in devs[:, 0]}) if hasattr(devs[0, 0], "coords") else 1
    cores = 2 if seq % 2 == 0 else 1
    return Mesh(devs.reshape(dp // ys, ys, seq // cores, cores), ("z", "y", "x", "c"))


def solution(mesh):
    fine = _split_mesh(mesh)
    rows = ("z", "y", "x", "c")
    placed = (
        P(rows, None),
        P(),
        P(rows, None),
        P(rows),
        P(),
        P(),
        P(("z", "y"), None, None),
    )
    return jax.shard_map(
        shards,
        mesh=fine,
        in_specs=placed,
        out_specs=(P(rows, None), P(("z", "y"), None, ("x", "c"))),
        check_vma=False,
    )
```

```python
import math

import jax
import jax.numpy as jnp
import numpy as np
from jax import lax
from jax.experimental import pallas as pl
from jax.experimental.pallas import tpu as pltpu
from jax.sharding import Mesh
from jax.sharding import PartitionSpec as P

D = 8192
KVW = 1024
HEAD_DIM = 128
BLK = 64
MOSTR = 6
SEQ_LEN = 1024
ROWS_PER_STEP = 8


def rope_back(grad, positions):
    heads = KVW // HEAD_DIM
    half = HEAD_DIM // 2
    values = grad.astype(jnp.float32).reshape(-1, heads, 2, half)
    freqs = 10000.0 ** (-2.0 * jnp.arange(half).astype(jnp.float32) / HEAD_DIM)
    angle = positions.astype(jnp.float32)[:, None] * freqs[None, :]
    cosine = jnp.cos(angle)[:, None, :]
    sine = jnp.sin(angle)[:, None, :]
    first = values[:, :, 0] * cosine + values[:, :, 1] * sine
    second = values[:, :, 1] * cosine - values[:, :, 0] * sine
    return jnp.stack([first, second], axis=2).reshape(-1, KVW).astype(jnp.bfloat16)


def _normed_grad_kernel(cols_ref, cnt_ref, gp_ref, bt_ref, out_ref, w_ref):
    step = pl.program_id(0)

    @pl.when(step == 0)
    def _():
        w_ref[...] = jnp.zeros(w_ref.shape, w_ref.dtype)

    def place(fill):
        for rr in range(ROWS_PER_STEP):
            row = step * ROWS_PER_STEP + rr
            live = cnt_ref[row]
            for k in range(MOSTR):
                start = pl.multiple_of(cols_ref[row * MOSTR + k] * BLK, BLK)
                if fill:
                    half = (k % 2) * BLK
                    value = bt_ref[rr, k // 2, :, half:half + BLK]
                    value = jnp.where(k < live, value, jnp.zeros_like(value))
                else:
                    value = jnp.zeros((BLK, BLK), w_ref.dtype)
                w_ref[pl.ds(start, BLK), rr * BLK:(rr + 1) * BLK] = value

    place(True)
    out_ref[...] = jnp.dot(gp_ref[...], w_ref[...], preferred_element_type=jnp.float32)
    place(False)


def normed_grad_of(grad_pre, blocks_t, cols, counts):
    tok = grad_pre.shape[0]
    row_blocks = blocks_t.shape[0]
    width = ROWS_PER_STEP * BLK
    spec = pltpu.PrefetchScalarGridSpec(
        num_scalar_prefetch=2,
        grid=(row_blocks // ROWS_PER_STEP,),
        in_specs=[
            pl.BlockSpec((tok, KVW), lambda g, c, n: (0, 0)),
            pl.BlockSpec((ROWS_PER_STEP, MOSTR // 2, BLK, 2 * BLK), lambda g, c, n: (g, 0, 0, 0)),
        ],
        out_specs=pl.BlockSpec((tok, width), lambda g, c, n: (0, g)),
        scratch_shapes=[pltpu.VMEM((KVW, width), jnp.bfloat16)],
    )
    return pl.pallas_call(
        _normed_grad_kernel,
        grid_spec=spec,
        out_shape=jax.ShapeDtypeStruct((tok, row_blocks * BLK), jnp.float32),
        compiler_params=pltpu.CompilerParams(dimension_semantics=("arbitrary",)),
    )(cols.reshape(-1), counts, grad_pre, blocks_t)


def shards(checkpoint, norm_gain, key_cotangent, positions, kept_cols, kept_count, key_blocks):
    tok_rows = checkpoint.shape[0]
    groups = lax.axis_size("x") * lax.axis_size("c")
    dp_size = lax.axis_size("z") * lax.axis_size("y")
    part_rows = BLK // groups
    row_blocks = D // BLK
    col_blocks = KVW // BLK
    xf = checkpoint.astype(jnp.float32)
    inv_rms = lax.rsqrt(jnp.mean(xf * xf, axis=1, keepdims=True) + 1e-05)
    normed = (xf * inv_rms * norm_gain).astype(jnp.bfloat16)
    grad_pre = rope_back(key_cotangent, positions)

    local_t = (
        key_blocks.reshape(key_blocks.shape[0], MOSTR // 2, 2, BLK, BLK)
        .transpose(0, 1, 4, 2, 3)
        .reshape(key_blocks.shape[0], MOSTR // 2, BLK, 2 * BLK)
    )
    piece = lax.all_gather(local_t, ("z", "y"), axis=0, tiled=True)

    split_normed = (
        normed.reshape(tok_rows, row_blocks, groups, part_rows)
        .transpose(0, 2, 1, 3)
        .reshape(tok_rows, groups, row_blocks * part_rows)
    )
    sent = jnp.concatenate(
        [split_normed, jnp.broadcast_to(grad_pre[:, None, :], (tok_rows, groups, KVW))], axis=2
    )
    received = lax.all_to_all(sent, ("x", "c"), split_axis=1, concat_axis=0, tiled=True)
    received = received.reshape(groups * tok_rows, row_blocks * part_rows + KVW)
    grad_all = received[:, row_blocks * part_rows:]
    normed_rows = received[:, : row_blocks * part_rows].reshape(groups * tok_rows, row_blocks, part_rows)
    divisor = math.sqrt(tok_rows * groups * dp_size)
    nz = lax.axis_size("z")
    ny = lax.axis_size("y")
    slab = normed_rows.reshape(groups * tok_rows, row_blocks * part_rows)
    product = lax.dot_general(
        grad_all, slab, (((0,), (0,)), ((), ())), preferred_element_type=jnp.float32
    )
    lanes = row_blocks * part_rows // nz
    blocks4 = product.reshape(col_blocks, BLK, nz, lanes)
    lane_row = (
        lax.broadcasted_iota(jnp.int32, (nz, lanes), 0) * lanes
        + lax.broadcasted_iota(jnp.int32, (nz, lanes), 1)
    ) // part_rows
    lane_cols = kept_cols[lane_row]
    lane_live = lax.broadcasted_iota(jnp.int32, (nz, lanes, MOSTR), 2) < kept_count[lane_row][:, :, None]
    partial = jnp.zeros((nz, MOSTR, BLK, lanes), jnp.float32)
    for c in range(col_blocks):
        hit = ((lane_cols == c) & lane_live).transpose(0, 2, 1)[:, :, None, :]
        partial = partial + jnp.where(hit, blocks4[c].transpose(1, 0, 2)[:, None, :, :], 0.0)
    partial = partial / divisor
    partial, piece = lax.optimization_barrier((partial, piece))
    summed = lax.psum_scatter(partial, "z", scatter_dimension=0, tiled=True)
    sub = lanes // ny
    summed = summed.reshape(MOSTR, BLK, ny, sub).transpose(2, 0, 3, 1)
    summed = lax.all_to_all(summed, "y", split_axis=0, concat_axis=0, tiled=True).sum(axis=0)
    own_rows = sub // part_rows
    block_grad = (
        summed.reshape(MOSTR, own_rows, part_rows, BLK)
        .transpose(1, 0, 2, 3)
        .reshape(own_rows, MOSTR, part_rows * BLK)
    )

    normed_grad = normed_grad_of(grad_pre, piece, kept_cols, kept_count)
    scaled = norm_gain * normed_grad
    grads = inv_rms * scaled - inv_rms**3 * xf * jnp.mean(scaled * xf, axis=1, keepdims=True)
    return (grads.astype(jnp.bfloat16), block_grad)


def _split_mesh(mesh):
    devs = mesh.devices
    dp, seq = devs.shape
    ys = len({d.coords[1] for d in devs[:, 0]}) if hasattr(devs[0, 0], "coords") else 1
    cores = 2 if seq % 2 == 0 else 1
    return Mesh(devs.reshape(dp // ys, ys, seq // cores, cores), ("z", "y", "x", "c"))


def solution(mesh):
    fine = _split_mesh(mesh)
    rows = ("z", "y", "x", "c")
    placed = (
        P(rows, None),
        P(),
        P(rows, None),
        P(rows),
        P(),
        P(),
        P(("z", "y"), None, None),
    )
    return jax.shard_map(
        shards,
        mesh=fine,
        in_specs=placed,
        out_specs=(P(rows, None), P(("z", "y"), None, ("x", "c"))),
        check_vma=False,
    )
```

```python
import functools
import math

import jax
import jax.numpy as jnp
import numpy as np
from jax import lax
from jax.experimental import pallas as pl
from jax.experimental.pallas import tpu as pltpu
from jax.sharding import Mesh
from jax.sharding import PartitionSpec as P

D = 8192
KVW = 1024
HEAD_DIM = 128
BLK = 64
MOSTR = 6
SEQ_LEN = 1024
ROWS_PER_STEP = 8


def rope_back(grad, positions):
    heads = KVW // HEAD_DIM
    half = HEAD_DIM // 2
    values = grad.astype(jnp.float32).reshape(-1, heads, 2, half)
    freqs = 10000.0 ** (-2.0 * jnp.arange(half).astype(jnp.float32) / HEAD_DIM)
    angle = positions.astype(jnp.float32)[:, None] * freqs[None, :]
    cosine = jnp.cos(angle)[:, None, :]
    sine = jnp.sin(angle)[:, None, :]
    first = values[:, :, 0] * cosine + values[:, :, 1] * sine
    second = values[:, :, 1] * cosine - values[:, :, 0] * sine
    return jnp.stack([first, second], axis=2).reshape(-1, KVW).astype(jnp.bfloat16)


def _normed_grad_kernel(cols_ref, cnt_ref, gp_ref, bt_ref, out_ref, w_ref):
    step = pl.program_id(0)

    @pl.when(step == 0)
    def _():
        w_ref[...] = jnp.zeros(w_ref.shape, w_ref.dtype)

    def place(fill):
        for rr in range(ROWS_PER_STEP):
            row = step * ROWS_PER_STEP + rr
            live = cnt_ref[row]
            for k in range(MOSTR):
                start = pl.multiple_of(cols_ref[row * MOSTR + k] * BLK, BLK)
                if fill:
                    half = (k % 2) * BLK
                    value = bt_ref[rr, k // 2, :, half:half + BLK]
                    value = jnp.where(k < live, value, jnp.zeros_like(value))
                else:
                    value = jnp.zeros((BLK, BLK), w_ref.dtype)
                w_ref[pl.ds(start, BLK), rr * BLK:(rr + 1) * BLK] = value

    place(True)
    out_ref[...] = jnp.dot(gp_ref[...], w_ref[...], preferred_element_type=jnp.float32)
    place(False)


def normed_grad_of(grad_pre, blocks_t, cols, counts):
    tok = grad_pre.shape[0]
    row_blocks = blocks_t.shape[0]
    width = ROWS_PER_STEP * BLK
    spec = pltpu.PrefetchScalarGridSpec(
        num_scalar_prefetch=2,
        grid=(row_blocks // ROWS_PER_STEP,),
        in_specs=[
            pl.BlockSpec((tok, KVW), lambda g, c, n: (0, 0)),
            pl.BlockSpec((ROWS_PER_STEP, MOSTR // 2, BLK, 2 * BLK), lambda g, c, n: (g, 0, 0, 0)),
        ],
        out_specs=pl.BlockSpec((tok, width), lambda g, c, n: (0, g)),
        scratch_shapes=[pltpu.VMEM((KVW, width), jnp.bfloat16)],
    )
    return pl.pallas_call(
        _normed_grad_kernel,
        grid_spec=spec,
        out_shape=jax.ShapeDtypeStruct((tok, row_blocks * BLK), jnp.float32),
        compiler_params=pltpu.CompilerParams(dimension_semantics=("arbitrary",)),
    )(cols.reshape(-1), counts, grad_pre, blocks_t)


def _pick_kernel(cols_ref, cnt_ref, pt_ref, out_ref, *, part_rows, divisor):
    step = pl.program_id(0)
    width = pt_ref.shape[1]
    per_step = width // part_rows
    group = lax.broadcasted_iota(jnp.int32, (BLK, width), 1) // part_rows
    for k in range(MOSTR):
        acc = jnp.zeros((BLK, width), jnp.float32)
        for rr in range(per_step):
            row = step * per_step + rr
            start = pl.multiple_of(cols_ref[row * MOSTR + k] * BLK, BLK)
            value = pt_ref[pl.ds(start, BLK), :]
            value = jnp.where(k < cnt_ref[row], value, jnp.zeros_like(value))
            acc = jnp.where(group == rr, value, acc)
        out_ref[0, k] = acc / divisor


def pick_blocks(product_t, cols, counts, part_rows, divisor):
    width = 128
    chunks = product_t.shape[1] // width
    spec = pltpu.PrefetchScalarGridSpec(
        num_scalar_prefetch=2,
        grid=(chunks,),
        in_specs=[pl.BlockSpec((product_t.shape[0], width), lambda g, c, n: (0, g))],
        out_specs=pl.BlockSpec((1, MOSTR, BLK, width), lambda g, c, n: (g, 0, 0, 0)),
    )
    return pl.pallas_call(
        functools.partial(_pick_kernel, part_rows=part_rows, divisor=divisor),
        grid_spec=spec,
        out_shape=jax.ShapeDtypeStruct((chunks, MOSTR, BLK, width), jnp.float32),
        compiler_params=pltpu.CompilerParams(dimension_semantics=("arbitrary",)),
    )(cols.reshape(-1), counts, product_t)


def shards(checkpoint, norm_gain, key_cotangent, positions, kept_cols, kept_count, key_blocks):
    tok_rows = checkpoint.shape[0]
    groups = lax.axis_size("x") * lax.axis_size("c")
    dp_size = lax.axis_size("z") * lax.axis_size("y")
    part_rows = BLK // groups
    row_blocks = D // BLK
    col_blocks = KVW // BLK
    xf = checkpoint.astype(jnp.float32)
    inv_rms = lax.rsqrt(jnp.mean(xf * xf, axis=1, keepdims=True) + 1e-05)
    normed = (xf * inv_rms * norm_gain).astype(jnp.bfloat16)
    grad_pre = rope_back(key_cotangent, positions)

    local_t = (
        key_blocks.reshape(key_blocks.shape[0], MOSTR // 2, 2, BLK, BLK)
        .transpose(0, 1, 4, 2, 3)
        .reshape(key_blocks.shape[0], MOSTR // 2, BLK, 2 * BLK)
    )
    piece = lax.all_gather(local_t, ("z", "y"), axis=0, tiled=True)

    split_normed = (
        normed.reshape(tok_rows, row_blocks, groups, part_rows)
        .transpose(0, 2, 1, 3)
        .reshape(tok_rows, groups, row_blocks * part_rows)
    )
    sent = jnp.concatenate(
        [split_normed, jnp.broadcast_to(grad_pre[:, None, :], (tok_rows, groups, KVW))], axis=2
    )
    received = lax.all_to_all(sent, ("x", "c"), split_axis=1, concat_axis=0, tiled=True)
    received = received.reshape(groups * tok_rows, row_blocks * part_rows + KVW)
    grad_all = received[:, row_blocks * part_rows:]
    normed_rows = received[:, : row_blocks * part_rows].reshape(groups * tok_rows, row_blocks, part_rows)
    divisor = math.sqrt(tok_rows * groups * dp_size)
    nz = lax.axis_size("z")
    ny = lax.axis_size("y")
    slab = normed_rows.reshape(groups * tok_rows, row_blocks * part_rows)
    product = lax.dot_general(
        grad_all, slab, (((0,), (0,)), ((), ())), preferred_element_type=jnp.float32
    )
    lanes = row_blocks * part_rows // nz
    partial = pick_blocks(product, kept_cols, kept_count, part_rows, divisor)
    partial, piece = lax.optimization_barrier((partial, piece))
    summed = lax.psum_scatter(partial, "z", scatter_dimension=0, tiled=True)
    sub = lanes // ny
    summed = summed.transpose(1, 2, 0, 3).reshape(MOSTR, BLK, ny, sub).transpose(2, 0, 3, 1)
    summed = lax.all_to_all(summed, "y", split_axis=0, concat_axis=0, tiled=True).sum(axis=0)
    own_rows = sub // part_rows
    block_grad = (
        summed.reshape(MOSTR, own_rows, part_rows, BLK)
        .transpose(1, 0, 2, 3)
        .reshape(own_rows, MOSTR, part_rows * BLK)
    )

    normed_grad = normed_grad_of(grad_pre, piece, kept_cols, kept_count)
    scaled = norm_gain * normed_grad
    grads = inv_rms * scaled - inv_rms**3 * xf * jnp.mean(scaled * xf, axis=1, keepdims=True)
    return (grads.astype(jnp.bfloat16), block_grad)


def _split_mesh(mesh):
    devs = mesh.devices
    dp, seq = devs.shape
    ys = len({d.coords[1] for d in devs[:, 0]}) if hasattr(devs[0, 0], "coords") else 1
    cores = 2 if seq % 2 == 0 else 1
    return Mesh(devs.reshape(dp // ys, ys, seq // cores, cores), ("z", "y", "x", "c"))


def solution(mesh):
    fine = _split_mesh(mesh)
    rows = ("z", "y", "x", "c")
    placed = (
        P(rows, None),
        P(),
        P(rows, None),
        P(rows),
        P(),
        P(),
        P(("z", "y"), None, None),
    )
    return jax.shard_map(
        shards,
        mesh=fine,
        in_specs=placed,
        out_specs=(P(rows, None), P(("z", "y"), None, ("x", "c"))),
        check_vma=False,
    )
```

```python
import functools
import math

import jax
import jax.numpy as jnp
import numpy as np
from jax import lax
from jax.experimental import pallas as pl
from jax.experimental.pallas import tpu as pltpu
from jax.sharding import Mesh
from jax.sharding import PartitionSpec as P

D = 8192
KVW = 1024
HEAD_DIM = 128
BLK = 64
MOSTR = 6
SEQ_LEN = 1024
ROWS_PER_STEP = 8


def rope_back(grad, positions):
    heads = KVW // HEAD_DIM
    half = HEAD_DIM // 2
    values = grad.astype(jnp.float32).reshape(-1, heads, 2, half)
    freqs = 10000.0 ** (-2.0 * jnp.arange(half).astype(jnp.float32) / HEAD_DIM)
    angle = positions.astype(jnp.float32)[:, None] * freqs[None, :]
    cosine = jnp.cos(angle)[:, None, :]
    sine = jnp.sin(angle)[:, None, :]
    first = values[:, :, 0] * cosine + values[:, :, 1] * sine
    second = values[:, :, 1] * cosine - values[:, :, 0] * sine
    return jnp.stack([first, second], axis=2).reshape(-1, KVW).astype(jnp.bfloat16)


def _normed_grad_kernel(cols_ref, cnt_ref, gp_ref, bt_ref, out_ref, w_ref):
    step = pl.program_id(0)

    @pl.when(step == 0)
    def _():
        w_ref[...] = jnp.zeros(w_ref.shape, w_ref.dtype)

    def place(fill):
        for rr in range(ROWS_PER_STEP):
            row = step * ROWS_PER_STEP + rr
            live = cnt_ref[row]
            for k in range(MOSTR):
                start = pl.multiple_of(cols_ref[row * MOSTR + k] * BLK, BLK)
                if fill:
                    half = (k % 2) * BLK
                    value = bt_ref[rr, k // 2, :, half:half + BLK]
                    value = jnp.where(k < live, value, jnp.zeros_like(value))
                else:
                    value = jnp.zeros((BLK, BLK), w_ref.dtype)
                w_ref[pl.ds(start, BLK), rr * BLK:(rr + 1) * BLK] = value

    place(True)
    out_ref[...] = jnp.dot(gp_ref[...], w_ref[...], preferred_element_type=jnp.float32)
    place(False)


def normed_grad_of(grad_pre, blocks_t, cols, counts):
    tok = grad_pre.shape[0]
    row_blocks = blocks_t.shape[0]
    width = ROWS_PER_STEP * BLK
    spec = pltpu.PrefetchScalarGridSpec(
        num_scalar_prefetch=2,
        grid=(row_blocks // ROWS_PER_STEP,),
        in_specs=[
            pl.BlockSpec((tok, KVW), lambda g, c, n: (0, 0)),
            pl.BlockSpec((ROWS_PER_STEP, MOSTR // 2, BLK, 2 * BLK), lambda g, c, n: (g, 0, 0, 0)),
        ],
        out_specs=pl.BlockSpec((tok, width), lambda g, c, n: (0, g)),
        scratch_shapes=[pltpu.VMEM((KVW, width), jnp.bfloat16)],
    )
    return pl.pallas_call(
        _normed_grad_kernel,
        grid_spec=spec,
        out_shape=jax.ShapeDtypeStruct((tok, row_blocks * BLK), jnp.float32),
        compiler_params=pltpu.CompilerParams(dimension_semantics=("arbitrary",)),
    )(cols.reshape(-1), counts, grad_pre, blocks_t)


def _pick_kernel(cols_ref, cnt_ref, pt_ref, out_ref, *, part_rows, divisor):
    step = pl.program_id(0)
    width = pt_ref.shape[1]
    per_step = width // part_rows
    dests = out_ref.shape[0]
    sub = width // dests
    group = lax.broadcasted_iota(jnp.int32, (BLK, width), 1) // part_rows
    for k in range(MOSTR):
        acc = jnp.zeros((BLK, width), jnp.float32)
        for rr in range(per_step):
            row = step * per_step + rr
            start = pl.multiple_of(cols_ref[row * MOSTR + k] * BLK, BLK)
            value = pt_ref[pl.ds(start, BLK), :]
            value = jnp.where(k < cnt_ref[row], value, jnp.zeros_like(value))
            acc = jnp.where(group == rr, value, acc)
        acc_t = (acc / divisor).T
        half = (k % 2) * BLK
        for d in range(dests):
            out_ref[d, k // 2, :, half:half + BLK] = acc_t[d * sub:(d + 1) * sub, :]


def pick_blocks(product_t, cols, counts, part_rows, divisor, devices):
    per_dev = product_t.shape[1] // devices
    width = max(128, per_dev)
    dests = width // per_dev
    chunks = product_t.shape[1] // width
    spec = pltpu.PrefetchScalarGridSpec(
        num_scalar_prefetch=2,
        grid=(chunks,),
        in_specs=[pl.BlockSpec((product_t.shape[0], width), lambda g, c, n: (0, g))],
        out_specs=pl.BlockSpec((dests, MOSTR // 2, per_dev, 2 * BLK), lambda g, c, n: (g, 0, 0, 0)),
    )
    return pl.pallas_call(
        functools.partial(_pick_kernel, part_rows=part_rows, divisor=divisor),
        grid_spec=spec,
        out_shape=jax.ShapeDtypeStruct((devices, MOSTR // 2, per_dev, 2 * BLK), jnp.float32),
        compiler_params=pltpu.CompilerParams(dimension_semantics=("arbitrary",)),
    )(cols.reshape(-1), counts, product_t)


def shards(checkpoint, norm_gain, key_cotangent, positions, kept_cols, kept_count, key_blocks):
    tok_rows = checkpoint.shape[0]
    groups = lax.axis_size("x") * lax.axis_size("c")
    dp_size = lax.axis_size("z") * lax.axis_size("y")
    part_rows = BLK // groups
    row_blocks = D // BLK
    col_blocks = KVW // BLK
    xf = checkpoint.astype(jnp.float32)
    inv_rms = lax.rsqrt(jnp.mean(xf * xf, axis=1, keepdims=True) + 1e-05)
    normed = (xf * inv_rms * norm_gain).astype(jnp.bfloat16)
    grad_pre = rope_back(key_cotangent, positions)

    local_t = (
        key_blocks.reshape(key_blocks.shape[0], MOSTR // 2, 2, BLK, BLK)
        .transpose(0, 1, 4, 2, 3)
        .reshape(key_blocks.shape[0], MOSTR // 2, BLK, 2 * BLK)
    )
    piece = lax.all_gather(local_t, ("z", "y"), axis=0, tiled=True)

    split_normed = (
        normed.reshape(tok_rows, row_blocks, groups, part_rows)
        .transpose(0, 2, 1, 3)
        .reshape(tok_rows, groups, row_blocks * part_rows)
    )
    sent = jnp.concatenate(
        [split_normed, jnp.broadcast_to(grad_pre[:, None, :], (tok_rows, groups, KVW))], axis=2
    )
    received = lax.all_to_all(sent, ("x", "c"), split_axis=1, concat_axis=0, tiled=True)
    received = received.reshape(groups * tok_rows, row_blocks * part_rows + KVW)
    grad_all = received[:, row_blocks * part_rows:]
    normed_rows = received[:, : row_blocks * part_rows].reshape(groups * tok_rows, row_blocks, part_rows)
    divisor = math.sqrt(tok_rows * groups * dp_size)
    slab = normed_rows.reshape(groups * tok_rows, row_blocks * part_rows)
    product = lax.dot_general(
        grad_all, slab, (((0,), (0,)), ((), ())), preferred_element_type=jnp.float32
    )
    partial = pick_blocks(product, kept_cols, kept_count, part_rows, divisor, dp_size)
    partial, piece = lax.optimization_barrier((partial, piece))
    summed = lax.all_to_all(partial, ("z", "y"), split_axis=0, concat_axis=0, tiled=True).sum(axis=0)
    own_rows = summed.shape[1] // part_rows
    block_grad = (
        summed.reshape(MOSTR // 2, own_rows, part_rows, 2, BLK)
        .transpose(1, 0, 3, 2, 4)
        .reshape(own_rows, MOSTR, part_rows * BLK)
    )

    normed_grad = normed_grad_of(grad_pre, piece, kept_cols, kept_count)
    scaled = norm_gain * normed_grad
    grads = inv_rms * scaled - inv_rms**3 * xf * jnp.mean(scaled * xf, axis=1, keepdims=True)
    return (grads.astype(jnp.bfloat16), block_grad)


def _split_mesh(mesh):
    devs = mesh.devices
    dp, seq = devs.shape
    ys = len({d.coords[1] for d in devs[:, 0]}) if hasattr(devs[0, 0], "coords") else 1
    cores = 2 if seq % 2 == 0 else 1
    return Mesh(devs.reshape(dp // ys, ys, seq // cores, cores), ("z", "y", "x", "c"))


def solution(mesh):
    fine = _split_mesh(mesh)
    rows = ("z", "y", "x", "c")
    placed = (
        P(rows, None),
        P(),
        P(rows, None),
        P(rows),
        P(),
        P(),
        P(("z", "y"), None, None),
    )
    return jax.shard_map(
        shards,
        mesh=fine,
        in_specs=placed,
        out_specs=(P(rows, None), P(("z", "y"), None, ("x", "c"))),
        check_vma=False,
    )
```

```python
import functools
import math

import jax
import jax.numpy as jnp
import numpy as np
from jax import lax
from jax.experimental import pallas as pl
from jax.experimental.pallas import tpu as pltpu
from jax.sharding import Mesh
from jax.sharding import PartitionSpec as P

D = 8192
KVW = 1024
HEAD_DIM = 128
BLK = 64
MOSTR = 6
SEQ_LEN = 1024
ROWS_PER_STEP = 8


def rope_back(grad, positions):
    heads = KVW // HEAD_DIM
    half = HEAD_DIM // 2
    values = grad.astype(jnp.float32).reshape(-1, heads, 2, half)
    freqs = 10000.0 ** (-2.0 * jnp.arange(half).astype(jnp.float32) / HEAD_DIM)
    angle = positions.astype(jnp.float32)[:, None] * freqs[None, :]
    cosine = jnp.cos(angle)[:, None, :]
    sine = jnp.sin(angle)[:, None, :]
    first = values[:, :, 0] * cosine + values[:, :, 1] * sine
    second = values[:, :, 1] * cosine - values[:, :, 0] * sine
    return jnp.stack([first, second], axis=2).reshape(-1, KVW).astype(jnp.bfloat16)


def _normed_grad_kernel(cols_ref, cnt_ref, gp_ref, bt_ref, out_ref, w_ref):
    step = pl.program_id(0)

    @pl.when(step == 0)
    def _():
        w_ref[...] = jnp.zeros(w_ref.shape, w_ref.dtype)

    def place(fill):
        for rr in range(ROWS_PER_STEP):
            row = step * ROWS_PER_STEP + rr
            live = cnt_ref[row]
            for k in range(MOSTR):
                start = pl.multiple_of(cols_ref[row * MOSTR + k] * BLK, BLK)
                if fill:
                    half = (k % 2) * BLK
                    value = bt_ref[rr, k // 2, :, half:half + BLK]
                    value = jnp.where(k < live, value, jnp.zeros_like(value))
                else:
                    value = jnp.zeros((BLK, BLK), w_ref.dtype)
                w_ref[pl.ds(start, BLK), rr * BLK:(rr + 1) * BLK] = value

    place(True)
    out_ref[...] = jnp.dot(gp_ref[...], w_ref[...], preferred_element_type=jnp.float32)
    place(False)


def normed_grad_of(grad_pre, blocks_t, cols, counts):
    tok = grad_pre.shape[0]
    row_blocks = blocks_t.shape[0]
    width = ROWS_PER_STEP * BLK
    spec = pltpu.PrefetchScalarGridSpec(
        num_scalar_prefetch=2,
        grid=(row_blocks // ROWS_PER_STEP,),
        in_specs=[
            pl.BlockSpec((tok, KVW), lambda g, c, n: (0, 0)),
            pl.BlockSpec((ROWS_PER_STEP, MOSTR // 2, BLK, 2 * BLK), lambda g, c, n: (g, 0, 0, 0)),
        ],
        out_specs=pl.BlockSpec((tok, width), lambda g, c, n: (0, g)),
        scratch_shapes=[pltpu.VMEM((KVW, width), jnp.bfloat16)],
    )
    return pl.pallas_call(
        _normed_grad_kernel,
        grid_spec=spec,
        out_shape=jax.ShapeDtypeStruct((tok, row_blocks * BLK), jnp.float32),
        compiler_params=pltpu.CompilerParams(dimension_semantics=("arbitrary",)),
    )(cols.reshape(-1), counts, grad_pre, blocks_t)


def _pick_kernel(cols_ref, cnt_ref, pt_ref, out_ref, *, part_rows, divisor):
    step = pl.program_id(0)
    width = pt_ref.shape[1]
    per_step = width // part_rows
    dests = out_ref.shape[0]
    sub = width // dests
    group = lax.broadcasted_iota(jnp.int32, (BLK, width), 1) // part_rows
    for k in range(MOSTR):
        acc = jnp.zeros((BLK, width), jnp.float32)
        for rr in range(per_step):
            row = step * per_step + rr
            start = pl.multiple_of(cols_ref[row * MOSTR + k] * BLK, BLK)
            value = pt_ref[pl.ds(start, BLK), :]
            value = jnp.where(k < cnt_ref[row], value, jnp.zeros_like(value))
            acc = jnp.where(group == rr, value, acc)
        acc_t = (acc / divisor).T
        half = (k % 2) * BLK
        for d in range(dests):
            out_ref[d, k // 2, :, half:half + BLK] = acc_t[d * sub:(d + 1) * sub, :].astype(out_ref.dtype)


def pick_blocks(product_t, cols, counts, part_rows, divisor, devices):
    per_dev = product_t.shape[1] // devices
    width = max(128, per_dev)
    dests = width // per_dev
    chunks = product_t.shape[1] // width
    spec = pltpu.PrefetchScalarGridSpec(
        num_scalar_prefetch=2,
        grid=(chunks,),
        in_specs=[pl.BlockSpec((product_t.shape[0], width), lambda g, c, n: (0, g))],
        out_specs=pl.BlockSpec((dests, MOSTR // 2, per_dev, 2 * BLK), lambda g, c, n: (g, 0, 0, 0)),
    )
    return pl.pallas_call(
        functools.partial(_pick_kernel, part_rows=part_rows, divisor=divisor),
        grid_spec=spec,
        out_shape=jax.ShapeDtypeStruct((devices, MOSTR // 2, per_dev, 2 * BLK), jnp.bfloat16),
        compiler_params=pltpu.CompilerParams(dimension_semantics=("arbitrary",)),
    )(cols.reshape(-1), counts, product_t)


def shards(checkpoint, norm_gain, key_cotangent, positions, kept_cols, kept_count, key_blocks):
    tok_rows = checkpoint.shape[0]
    groups = lax.axis_size("x") * lax.axis_size("c")
    dp_size = lax.axis_size("z") * lax.axis_size("y")
    part_rows = BLK // groups
    row_blocks = D // BLK
    col_blocks = KVW // BLK
    xf = checkpoint.astype(jnp.float32)
    inv_rms = lax.rsqrt(jnp.mean(xf * xf, axis=1, keepdims=True) + 1e-05)
    normed = (xf * inv_rms * norm_gain).astype(jnp.bfloat16)
    grad_pre = rope_back(key_cotangent, positions)

    local_t = (
        key_blocks.reshape(key_blocks.shape[0], MOSTR // 2, 2, BLK, BLK)
        .transpose(0, 1, 4, 2, 3)
        .reshape(key_blocks.shape[0], MOSTR // 2, BLK, 2 * BLK)
    )
    piece = lax.all_gather(local_t, ("z", "y"), axis=0, tiled=True)

    split_normed = (
        normed.reshape(tok_rows, row_blocks, groups, part_rows)
        .transpose(0, 2, 1, 3)
        .reshape(tok_rows, groups, row_blocks * part_rows)
    )
    sent = jnp.concatenate(
        [split_normed, jnp.broadcast_to(grad_pre[:, None, :], (tok_rows, groups, KVW))], axis=2
    )
    received = lax.all_to_all(sent, ("x", "c"), split_axis=1, concat_axis=0, tiled=True)
    received = received.reshape(groups * tok_rows, row_blocks * part_rows + KVW)
    grad_all = received[:, row_blocks * part_rows:]
    normed_rows = received[:, : row_blocks * part_rows].reshape(groups * tok_rows, row_blocks, part_rows)
    divisor = math.sqrt(tok_rows * groups * dp_size)
    slab = normed_rows.reshape(groups * tok_rows, row_blocks * part_rows)
    product = lax.dot_general(
        grad_all, slab, (((0,), (0,)), ((), ())), preferred_element_type=jnp.float32
    )
    partial = pick_blocks(product, kept_cols, kept_count, part_rows, divisor, dp_size)
    partial, piece = lax.optimization_barrier((partial, piece))
    summed = lax.all_to_all(partial, ("z", "y"), split_axis=0, concat_axis=0, tiled=True)
    summed = summed.astype(jnp.float32).sum(axis=0)
    own_rows = summed.shape[1] // part_rows
    block_grad = (
        summed.reshape(MOSTR // 2, own_rows, part_rows, 2, BLK)
        .transpose(1, 0, 3, 2, 4)
        .reshape(own_rows, MOSTR, part_rows * BLK)
    )

    normed_grad = normed_grad_of(grad_pre, piece, kept_cols, kept_count)
    scaled = norm_gain * normed_grad
    grads = inv_rms * scaled - inv_rms**3 * xf * jnp.mean(scaled * xf, axis=1, keepdims=True)
    return (grads.astype(jnp.bfloat16), block_grad)


def _split_mesh(mesh):
    devs = mesh.devices
    dp, seq = devs.shape
    ys = len({d.coords[1] for d in devs[:, 0]}) if hasattr(devs[0, 0], "coords") else 1
    cores = 2 if seq % 2 == 0 else 1
    return Mesh(devs.reshape(dp // ys, ys, seq // cores, cores), ("z", "y", "x", "c"))


def solution(mesh):
    fine = _split_mesh(mesh)
    rows = ("z", "y", "x", "c")
    placed = (
        P(rows, None),
        P(),
        P(rows, None),
        P(rows),
        P(),
        P(),
        P(("z", "y"), None, None),
    )
    return jax.shard_map(
        shards,
        mesh=fine,
        in_specs=placed,
        out_specs=(P(rows, None), P(("z", "y"), None, ("x", "c"))),
        check_vma=False,
    )
```

```python
import functools
import math

import jax
import jax.numpy as jnp
import numpy as np
from jax import lax
from jax.experimental import pallas as pl
from jax.experimental.pallas import tpu as pltpu
from jax.sharding import Mesh
from jax.sharding import PartitionSpec as P

D = 8192
KVW = 1024
HEAD_DIM = 128
BLK = 64
MOSTR = 6
SEQ_LEN = 1024
ROWS_PER_STEP = 8


def rope_back(grad, positions):
    heads = KVW // HEAD_DIM
    half = HEAD_DIM // 2
    values = grad.astype(jnp.float32).reshape(-1, heads, 2, half)
    freqs = 10000.0 ** (-2.0 * jnp.arange(half).astype(jnp.float32) / HEAD_DIM)
    angle = positions.astype(jnp.float32)[:, None] * freqs[None, :]
    cosine = jnp.cos(angle)[:, None, :]
    sine = jnp.sin(angle)[:, None, :]
    first = values[:, :, 0] * cosine + values[:, :, 1] * sine
    second = values[:, :, 1] * cosine - values[:, :, 0] * sine
    return jnp.stack([first, second], axis=2).reshape(-1, KVW).astype(jnp.bfloat16)


def _normed_grad_kernel(cols_ref, cnt_ref, core_ref, gp_ref, own_ref, other_ref, out_ref, w_ref):
    step = pl.program_id(0)
    rows = own_ref.shape[2]
    own_at = core_ref[0] * rows
    other_at = (1 - core_ref[0]) * rows

    @pl.when(step == 0)
    def _():
        w_ref[...] = jnp.zeros(w_ref.shape, w_ref.dtype)

    def place(fill):
        for rr in range(ROWS_PER_STEP):
            row = step * ROWS_PER_STEP + rr
            live = cnt_ref[row]
            lanes = slice(rr * BLK, (rr + 1) * BLK)
            for k in range(MOSTR):
                start = cols_ref[row * MOSTR + k] * BLK
                if fill:
                    half = (k % 2) * BLK
                    for at, ref in ((own_at, own_ref), (other_at, other_ref)):
                        value = ref[rr, k // 2, :, half:half + BLK]
                        value = jnp.where(k < live, value, jnp.zeros_like(value))
                        w_ref[pl.ds(pl.multiple_of(start + at, rows), rows), lanes] = value
                else:
                    zero = jnp.zeros((BLK, BLK), w_ref.dtype)
                    w_ref[pl.ds(pl.multiple_of(start, BLK), BLK), lanes] = zero

    place(True)
    out_ref[...] = jnp.dot(gp_ref[...], w_ref[...], preferred_element_type=jnp.float32)
    place(False)


def normed_grad_of(grad_pre, own, other, core, cols, counts):
    tok = grad_pre.shape[0]
    row_blocks = own.shape[0]
    rows = own.shape[2]
    width = ROWS_PER_STEP * BLK
    half_spec = pl.BlockSpec((ROWS_PER_STEP, MOSTR // 2, rows, 2 * BLK), lambda g, c, n, h: (g, 0, 0, 0))
    spec = pltpu.PrefetchScalarGridSpec(
        num_scalar_prefetch=3,
        grid=(row_blocks // ROWS_PER_STEP,),
        in_specs=[pl.BlockSpec((tok, KVW), lambda g, c, n, h: (0, 0)), half_spec, half_spec],
        out_specs=pl.BlockSpec((tok, width), lambda g, c, n, h: (0, g)),
        scratch_shapes=[pltpu.VMEM((KVW, width), jnp.bfloat16)],
    )
    return pl.pallas_call(
        _normed_grad_kernel,
        grid_spec=spec,
        out_shape=jax.ShapeDtypeStruct((tok, row_blocks * BLK), jnp.float32),
        compiler_params=pltpu.CompilerParams(dimension_semantics=("arbitrary",)),
    )(cols.reshape(-1), counts, core, grad_pre, own, other)


def _pick_kernel(cols_ref, cnt_ref, pt_ref, out_ref, *, part_rows, divisor):
    step = pl.program_id(0)
    width = pt_ref.shape[1]
    per_step = width // part_rows
    dests = out_ref.shape[0]
    sub = width // dests
    group = lax.broadcasted_iota(jnp.int32, (BLK, width), 1) // part_rows
    for k in range(MOSTR):
        acc = jnp.zeros((BLK, width), jnp.float32)
        for rr in range(per_step):
            row = step * per_step + rr
            start = pl.multiple_of(cols_ref[row * MOSTR + k] * BLK, BLK)
            value = pt_ref[pl.ds(start, BLK), :]
            value = jnp.where(k < cnt_ref[row], value, jnp.zeros_like(value))
            acc = jnp.where(group == rr, value, acc)
        acc_t = (acc / divisor).T
        half = (k % 2) * BLK
        for d in range(dests):
            out_ref[d, k // 2, :, half:half + BLK] = acc_t[d * sub:(d + 1) * sub, :].astype(out_ref.dtype)


def pick_blocks(product_t, cols, counts, part_rows, divisor, devices):
    per_dev = product_t.shape[1] // devices
    width = max(128, per_dev)
    dests = width // per_dev
    chunks = product_t.shape[1] // width
    spec = pltpu.PrefetchScalarGridSpec(
        num_scalar_prefetch=2,
        grid=(chunks,),
        in_specs=[pl.BlockSpec((product_t.shape[0], width), lambda g, c, n: (0, g))],
        out_specs=pl.BlockSpec((dests, MOSTR // 2, per_dev, 2 * BLK), lambda g, c, n: (g, 0, 0, 0)),
    )
    return pl.pallas_call(
        functools.partial(_pick_kernel, part_rows=part_rows, divisor=divisor),
        grid_spec=spec,
        out_shape=jax.ShapeDtypeStruct((devices, MOSTR // 2, per_dev, 2 * BLK), jnp.bfloat16),
        compiler_params=pltpu.CompilerParams(dimension_semantics=("arbitrary",)),
    )(cols.reshape(-1), counts, product_t)


def shards(checkpoint, norm_gain, key_cotangent, positions, kept_cols, kept_count, key_blocks):
    tok_rows = checkpoint.shape[0]
    groups = lax.axis_size("x") * lax.axis_size("c")
    dp_size = lax.axis_size("z") * lax.axis_size("y")
    part_rows = BLK // groups
    row_blocks = D // BLK
    col_blocks = KVW // BLK
    xf = checkpoint.astype(jnp.float32)
    inv_rms = lax.rsqrt(jnp.mean(xf * xf, axis=1, keepdims=True) + 1e-05)
    normed = (xf * inv_rms * norm_gain).astype(jnp.bfloat16)
    grad_pre = rope_back(key_cotangent, positions)

    local_t = (
        key_blocks.reshape(key_blocks.shape[0], MOSTR // 2, 2, BLK, BLK)
        .transpose(0, 1, 4, 2, 3)
        .reshape(key_blocks.shape[0], MOSTR // 2, BLK, 2 * BLK)
    )
    cores = lax.axis_size("c")
    core = lax.axis_index("c")
    half_rows = BLK // cores
    local_h = lax.dynamic_slice_in_dim(local_t, core * half_rows, half_rows, axis=2)
    own = lax.all_gather(local_h, ("z", "y"), axis=0, tiled=True)
    other = lax.ppermute(own, "c", perm=[(i, (i + 1) % cores) for i in range(cores)])

    split_normed = (
        normed.reshape(tok_rows, row_blocks, groups, part_rows)
        .transpose(0, 2, 1, 3)
        .reshape(tok_rows, groups, row_blocks * part_rows)
    )
    sent = jnp.concatenate(
        [split_normed, jnp.broadcast_to(grad_pre[:, None, :], (tok_rows, groups, KVW))], axis=2
    )
    received = lax.all_to_all(sent, ("x", "c"), split_axis=1, concat_axis=0, tiled=True)
    received = received.reshape(groups * tok_rows, row_blocks * part_rows + KVW)
    normed_grad = normed_grad_of(grad_pre, own, other, core.reshape(1), kept_cols, kept_count)
    normed_grad, received = lax.optimization_barrier((normed_grad, received))
    grad_all = received[:, row_blocks * part_rows:]
    normed_rows = received[:, : row_blocks * part_rows].reshape(groups * tok_rows, row_blocks, part_rows)
    divisor = math.sqrt(tok_rows * groups * dp_size)
    slab = normed_rows.reshape(groups * tok_rows, row_blocks * part_rows)
    product = lax.dot_general(
        grad_all, slab, (((0,), (0,)), ((), ())), preferred_element_type=jnp.float32
    )
    partial = pick_blocks(product, kept_cols, kept_count, part_rows, divisor, dp_size)
    summed = lax.all_to_all(partial, ("z", "y"), split_axis=0, concat_axis=0, tiled=True)
    summed = summed.astype(jnp.float32).sum(axis=0)
    own_rows = summed.shape[1] // part_rows
    block_grad = (
        summed.reshape(MOSTR // 2, own_rows, part_rows, 2, BLK)
        .transpose(1, 0, 3, 2, 4)
        .reshape(own_rows, MOSTR, part_rows * BLK)
    )

    scaled = norm_gain * normed_grad
    grads = inv_rms * scaled - inv_rms**3 * xf * jnp.mean(scaled * xf, axis=1, keepdims=True)
    return (grads.astype(jnp.bfloat16), block_grad)


def _split_mesh(mesh):
    devs = mesh.devices
    dp, seq = devs.shape
    ys = len({d.coords[1] for d in devs[:, 0]}) if hasattr(devs[0, 0], "coords") else 1
    cores = 2 if seq % 2 == 0 else 1
    return Mesh(devs.reshape(dp // ys, ys, seq // cores, cores), ("z", "y", "x", "c"))


def solution(mesh):
    fine = _split_mesh(mesh)
    rows = ("z", "y", "x", "c")
    placed = (
        P(rows, None),
        P(),
        P(rows, None),
        P(rows),
        P(),
        P(),
        P(("z", "y"), None, None),
    )
    return jax.shard_map(
        shards,
        mesh=fine,
        in_specs=placed,
        out_specs=(P(rows, None), P(("z", "y"), None, ("x", "c"))),
        check_vma=False,
    )
```

```python
import functools
import math

import jax
import jax.numpy as jnp
import numpy as np
from jax import lax
from jax.experimental import pallas as pl
from jax.experimental.pallas import tpu as pltpu
from jax.sharding import Mesh
from jax.sharding import PartitionSpec as P

D = 8192
KVW = 1024
HEAD_DIM = 128
BLK = 64
MOSTR = 6
SEQ_LEN = 1024
ROWS_PER_STEP = 8


def rope_back(grad, positions):
    heads = KVW // HEAD_DIM
    half = HEAD_DIM // 2
    values = grad.astype(jnp.float32).reshape(-1, heads, 2, half)
    freqs = 10000.0 ** (-2.0 * jnp.arange(half).astype(jnp.float32) / HEAD_DIM)
    angle = positions.astype(jnp.float32)[:, None] * freqs[None, :]
    cosine = jnp.cos(angle)[:, None, :]
    sine = jnp.sin(angle)[:, None, :]
    first = values[:, :, 0] * cosine + values[:, :, 1] * sine
    second = values[:, :, 1] * cosine - values[:, :, 0] * sine
    return jnp.stack([first, second], axis=2).reshape(-1, KVW).astype(jnp.bfloat16)


def _normed_grad_kernel(cols_ref, cnt_ref, gp_ref, bt_ref, out_ref, w_ref):
    step = pl.program_id(0)

    @pl.when(step == 0)
    def _():
        w_ref[...] = jnp.zeros(w_ref.shape, w_ref.dtype)

    def place(fill):
        for rr in range(ROWS_PER_STEP):
            row = step * ROWS_PER_STEP + rr
            live = cnt_ref[row]
            for k in range(MOSTR):
                start = pl.multiple_of(cols_ref[row * MOSTR + k] * BLK, BLK)
                if fill:
                    half = (k % 2) * BLK
                    value = bt_ref[rr, k // 2, :, half:half + BLK]
                    value = jnp.where(k < live, value, jnp.zeros_like(value))
                else:
                    value = jnp.zeros((BLK, BLK), w_ref.dtype)
                w_ref[pl.ds(start, BLK), rr * BLK:(rr + 1) * BLK] = value

    place(True)
    out_ref[...] = jnp.dot(gp_ref[...], w_ref[...], preferred_element_type=jnp.float32)
    place(False)


def normed_grad_of(grad_pre, blocks_t, cols, counts):
    tok = grad_pre.shape[0]
    row_blocks = blocks_t.shape[0]
    width = ROWS_PER_STEP * BLK
    spec = pltpu.PrefetchScalarGridSpec(
        num_scalar_prefetch=2,
        grid=(row_blocks // ROWS_PER_STEP,),
        in_specs=[
            pl.BlockSpec((tok, KVW), lambda g, c, n: (0, 0)),
            pl.BlockSpec((ROWS_PER_STEP, MOSTR // 2, BLK, 2 * BLK), lambda g, c, n: (g, 0, 0, 0)),
        ],
        out_specs=pl.BlockSpec((tok, width), lambda g, c, n: (0, g)),
        scratch_shapes=[pltpu.VMEM((KVW, width), jnp.bfloat16)],
    )
    return pl.pallas_call(
        _normed_grad_kernel,
        grid_spec=spec,
        out_shape=jax.ShapeDtypeStruct((tok, row_blocks * BLK), jnp.float32),
        compiler_params=pltpu.CompilerParams(dimension_semantics=("arbitrary",)),
    )(cols.reshape(-1), counts, grad_pre, blocks_t)


def _pick_kernel(cols_ref, cnt_ref, pt_ref, out_ref, *, part_rows, divisor):
    step = pl.program_id(0)
    width = pt_ref.shape[1]
    per_step = width // part_rows
    dests = out_ref.shape[0]
    sub = width // dests
    group = lax.broadcasted_iota(jnp.int32, (BLK, width), 1) // part_rows
    for k in range(MOSTR):
        acc = jnp.zeros((BLK, width), jnp.float32)
        for rr in range(per_step):
            row = step * per_step + rr
            start = pl.multiple_of(cols_ref[row * MOSTR + k] * BLK, BLK)
            value = pt_ref[pl.ds(start, BLK), :]
            value = jnp.where(k < cnt_ref[row], value, jnp.zeros_like(value))
            acc = jnp.where(group == rr, value, acc)
        acc_t = (acc / divisor).T
        half = (k % 2) * BLK
        for d in range(dests):
            out_ref[d, k // 2, :, half:half + BLK] = acc_t[d * sub:(d + 1) * sub, :].astype(out_ref.dtype)


def pick_blocks(product_t, cols, counts, part_rows, divisor, devices):
    per_dev = product_t.shape[1] // devices
    width = max(128, per_dev)
    dests = width // per_dev
    chunks = product_t.shape[1] // width
    spec = pltpu.PrefetchScalarGridSpec(
        num_scalar_prefetch=2,
        grid=(chunks,),
        in_specs=[pl.BlockSpec((product_t.shape[0], width), lambda g, c, n: (0, g))],
        out_specs=pl.BlockSpec((dests, MOSTR // 2, per_dev, 2 * BLK), lambda g, c, n: (g, 0, 0, 0)),
    )
    return pl.pallas_call(
        functools.partial(_pick_kernel, part_rows=part_rows, divisor=divisor),
        grid_spec=spec,
        out_shape=jax.ShapeDtypeStruct((devices, MOSTR // 2, per_dev, 2 * BLK), jnp.bfloat16),
        compiler_params=pltpu.CompilerParams(dimension_semantics=("arbitrary",)),
    )(cols.reshape(-1), counts, product_t)


def shards(checkpoint, norm_gain, key_cotangent, positions, kept_cols, kept_count, key_blocks):
    tok_rows = checkpoint.shape[0]
    groups = lax.axis_size("x") * lax.axis_size("c")
    dp_size = lax.axis_size("z") * lax.axis_size("y")
    part_rows = BLK // groups
    row_blocks = D // BLK
    col_blocks = KVW // BLK
    xf = checkpoint.astype(jnp.float32)
    inv_rms = lax.rsqrt(jnp.mean(xf * xf, axis=1, keepdims=True) + 1e-05)
    normed = (xf * inv_rms * norm_gain).astype(jnp.bfloat16)
    grad_pre = rope_back(key_cotangent, positions)

    local_t = (
        key_blocks.reshape(key_blocks.shape[0], MOSTR // 2, 2, BLK, BLK)
        .transpose(0, 1, 4, 2, 3)
        .reshape(key_blocks.shape[0], MOSTR // 2, BLK, 2 * BLK)
    )
    piece = lax.all_gather(local_t, ("z", "y"), axis=0, tiled=True)

    split_normed = (
        normed.reshape(tok_rows, row_blocks, groups, part_rows)
        .transpose(0, 2, 1, 3)
        .reshape(tok_rows, groups, row_blocks * part_rows)
    )
    sent = jnp.concatenate(
        [split_normed, jnp.broadcast_to(grad_pre[:, None, :], (tok_rows, groups, KVW))], axis=2
    )
    received = lax.all_to_all(sent, ("x", "c"), split_axis=1, concat_axis=0, tiled=True)
    received = received.reshape(groups * tok_rows, row_blocks * part_rows + KVW)
    grad_all = received[:, row_blocks * part_rows:]
    normed_rows = received[:, : row_blocks * part_rows].reshape(groups * tok_rows, row_blocks, part_rows)
    divisor = math.sqrt(tok_rows * groups * dp_size)
    slab = normed_rows.reshape(groups * tok_rows, row_blocks * part_rows)
    product = lax.dot_general(
        grad_all, slab, (((0,), (0,)), ((), ())), preferred_element_type=jnp.float32
    )
    partial = pick_blocks(product, kept_cols, kept_count, part_rows, divisor, dp_size)
    partial, piece = lax.optimization_barrier((partial, piece))
    summed = lax.all_to_all(partial, ("z", "y"), split_axis=0, concat_axis=0, tiled=True)
    normed_grad = normed_grad_of(grad_pre, piece, kept_cols, kept_count)
    scaled = norm_gain * normed_grad
    grads = inv_rms * scaled - inv_rms**3 * xf * jnp.mean(scaled * xf, axis=1, keepdims=True)
    grads = grads.astype(jnp.bfloat16)
    summed, grads = lax.optimization_barrier((summed, grads))
    summed = summed.astype(jnp.float32).sum(axis=0)
    own_rows = summed.shape[1] // part_rows
    block_grad = (
        summed.reshape(MOSTR // 2, own_rows, part_rows, 2, BLK)
        .transpose(1, 0, 3, 2, 4)
        .reshape(own_rows, MOSTR, part_rows * BLK)
    )

    return (grads, block_grad)


def _split_mesh(mesh):
    devs = mesh.devices
    dp, seq = devs.shape
    ys = len({d.coords[1] for d in devs[:, 0]}) if hasattr(devs[0, 0], "coords") else 1
    cores = 2 if seq % 2 == 0 else 1
    return Mesh(devs.reshape(dp // ys, ys, seq // cores, cores), ("z", "y", "x", "c"))


def solution(mesh):
    fine = _split_mesh(mesh)
    rows = ("z", "y", "x", "c")
    placed = (
        P(rows, None),
        P(),
        P(rows, None),
        P(rows),
        P(),
        P(),
        P(("z", "y"), None, None),
    )
    return jax.shard_map(
        shards,
        mesh=fine,
        in_specs=placed,
        out_specs=(P(rows, None), P(("z", "y"), None, ("x", "c"))),
        check_vma=False,
    )
```

```python
import functools
import math

import jax
import jax.numpy as jnp
import numpy as np
from jax import lax
from jax.experimental import pallas as pl
from jax.experimental.pallas import tpu as pltpu
from jax.sharding import Mesh
from jax.sharding import PartitionSpec as P

D = 8192
KVW = 1024
HEAD_DIM = 128
BLK = 64
MOSTR = 6
SEQ_LEN = 1024
ROWS_PER_STEP = 16


def rope_back(grad, positions):
    heads = KVW // HEAD_DIM
    half = HEAD_DIM // 2
    values = grad.astype(jnp.float32).reshape(-1, heads, 2, half)
    freqs = 10000.0 ** (-2.0 * jnp.arange(half).astype(jnp.float32) / HEAD_DIM)
    angle = positions.astype(jnp.float32)[:, None] * freqs[None, :]
    cosine = jnp.cos(angle)[:, None, :]
    sine = jnp.sin(angle)[:, None, :]
    first = values[:, :, 0] * cosine + values[:, :, 1] * sine
    second = values[:, :, 1] * cosine - values[:, :, 0] * sine
    return jnp.stack([first, second], axis=2).reshape(-1, KVW).astype(jnp.bfloat16)


def _normed_grad_kernel(cols_ref, cnt_ref, gp_ref, bt_ref, out_ref, w_ref):
    step = pl.program_id(0)

    @pl.when(step == 0)
    def _():
        w_ref[...] = jnp.zeros(w_ref.shape, w_ref.dtype)

    def place(fill):
        for rr in range(ROWS_PER_STEP):
            row = step * ROWS_PER_STEP + rr
            live = cnt_ref[row]
            for k in range(MOSTR):
                start = pl.multiple_of(cols_ref[row * MOSTR + k] * BLK, BLK)
                if fill:
                    half = (k % 2) * BLK
                    value = bt_ref[rr, k // 2, :, half:half + BLK]
                    value = jnp.where(k < live, value, jnp.zeros_like(value))
                else:
                    value = jnp.zeros((BLK, BLK), w_ref.dtype)
                w_ref[pl.ds(start, BLK), rr * BLK:(rr + 1) * BLK] = value

    place(True)
    out_ref[...] = jnp.dot(gp_ref[...], w_ref[...], preferred_element_type=jnp.float32)
    place(False)


def normed_grad_of(grad_pre, blocks_t, cols, counts):
    tok = grad_pre.shape[0]
    row_blocks = blocks_t.shape[0]
    width = ROWS_PER_STEP * BLK
    spec = pltpu.PrefetchScalarGridSpec(
        num_scalar_prefetch=2,
        grid=(row_blocks // ROWS_PER_STEP,),
        in_specs=[
            pl.BlockSpec((tok, KVW), lambda g, c, n: (0, 0)),
            pl.BlockSpec((ROWS_PER_STEP, MOSTR // 2, BLK, 2 * BLK), lambda g, c, n: (g, 0, 0, 0)),
        ],
        out_specs=pl.BlockSpec((tok, width), lambda g, c, n: (0, g)),
        scratch_shapes=[pltpu.VMEM((KVW, width), jnp.bfloat16)],
    )
    return pl.pallas_call(
        _normed_grad_kernel,
        grid_spec=spec,
        out_shape=jax.ShapeDtypeStruct((tok, row_blocks * BLK), jnp.float32),
        compiler_params=pltpu.CompilerParams(dimension_semantics=("arbitrary",)),
    )(cols.reshape(-1), counts, grad_pre, blocks_t)


def _pick_kernel(cols_ref, cnt_ref, pt_ref, out_ref, *, part_rows, divisor):
    step = pl.program_id(0)
    width = pt_ref.shape[1]
    per_step = width // part_rows
    dests = out_ref.shape[0]
    sub = width // dests
    group = lax.broadcasted_iota(jnp.int32, (BLK, width), 1) // part_rows
    for k in range(MOSTR):
        acc = jnp.zeros((BLK, width), jnp.float32)
        for rr in range(per_step):
            row = step * per_step + rr
            start = pl.multiple_of(cols_ref[row * MOSTR + k] * BLK, BLK)
            acc = jnp.where(group == rr, pt_ref[pl.ds(start, BLK), :], acc)
        acc_t = (acc / divisor).T
        half = (k % 2) * BLK
        for d in range(dests):
            out_ref[d, k // 2, :, half:half + BLK] = acc_t[d * sub:(d + 1) * sub, :].astype(out_ref.dtype)


def pick_blocks(product_t, cols, counts, part_rows, divisor, devices):
    per_dev = product_t.shape[1] // devices
    width = max(128, per_dev)
    dests = width // per_dev
    chunks = product_t.shape[1] // width
    spec = pltpu.PrefetchScalarGridSpec(
        num_scalar_prefetch=2,
        grid=(chunks,),
        in_specs=[pl.BlockSpec((product_t.shape[0], width), lambda g, c, n: (0, g))],
        out_specs=pl.BlockSpec((dests, MOSTR // 2, per_dev, 2 * BLK), lambda g, c, n: (g, 0, 0, 0)),
    )
    return pl.pallas_call(
        functools.partial(_pick_kernel, part_rows=part_rows, divisor=divisor),
        grid_spec=spec,
        out_shape=jax.ShapeDtypeStruct((devices, MOSTR // 2, per_dev, 2 * BLK), jnp.bfloat16),
        compiler_params=pltpu.CompilerParams(dimension_semantics=("arbitrary",)),
    )(cols.reshape(-1), counts, product_t)


def shards(checkpoint, norm_gain, key_cotangent, positions, kept_cols, kept_count, key_blocks):
    tok_rows = checkpoint.shape[0]
    groups = lax.axis_size("x") * lax.axis_size("c")
    dp_size = lax.axis_size("z") * lax.axis_size("y")
    part_rows = BLK // groups
    row_blocks = D // BLK
    col_blocks = KVW // BLK
    xf = checkpoint.astype(jnp.float32)
    inv_rms = lax.rsqrt(jnp.mean(xf * xf, axis=1, keepdims=True) + 1e-05)
    normed = (xf * inv_rms * norm_gain).astype(jnp.bfloat16)
    grad_pre = rope_back(key_cotangent, positions)

    local_t = (
        key_blocks.reshape(key_blocks.shape[0], MOSTR // 2, 2, BLK, BLK)
        .transpose(0, 1, 4, 2, 3)
        .reshape(key_blocks.shape[0], MOSTR // 2, BLK, 2 * BLK)
    )
    piece = lax.all_gather(local_t, ("z", "y"), axis=0, tiled=True)

    split_normed = (
        normed.reshape(tok_rows, row_blocks, groups, part_rows)
        .transpose(0, 2, 1, 3)
        .reshape(tok_rows, groups, row_blocks * part_rows)
    )
    sent = jnp.concatenate(
        [split_normed, jnp.broadcast_to(grad_pre[:, None, :], (tok_rows, groups, KVW))], axis=2
    )
    received = lax.all_to_all(sent, ("x", "c"), split_axis=1, concat_axis=0, tiled=True)
    received = received.reshape(groups * tok_rows, row_blocks * part_rows + KVW)
    grad_all = received[:, row_blocks * part_rows:]
    normed_rows = received[:, : row_blocks * part_rows].reshape(groups * tok_rows, row_blocks, part_rows)
    divisor = math.sqrt(tok_rows * groups * dp_size)
    slab = normed_rows.reshape(groups * tok_rows, row_blocks * part_rows)
    product = lax.dot_general(
        grad_all, slab, (((0,), (0,)), ((), ())), preferred_element_type=jnp.float32
    )
    partial = pick_blocks(product, kept_cols, kept_count, part_rows, divisor, dp_size)
    partial, piece = lax.optimization_barrier((partial, piece))
    summed = lax.all_to_all(partial, ("z", "y"), split_axis=0, concat_axis=0, tiled=True)
    normed_grad = normed_grad_of(grad_pre, piece, kept_cols, kept_count)
    scaled = norm_gain * normed_grad
    grads = inv_rms * scaled - inv_rms**3 * xf * jnp.mean(scaled * xf, axis=1, keepdims=True)
    grads = grads.astype(jnp.bfloat16)
    summed, grads = lax.optimization_barrier((summed, grads))
    summed = summed.astype(jnp.float32).sum(axis=0)
    own_rows = summed.shape[1] // part_rows
    block_grad = (
        summed.reshape(MOSTR // 2, own_rows, part_rows, 2, BLK)
        .transpose(1, 0, 3, 2, 4)
        .reshape(own_rows, MOSTR, part_rows * BLK)
    )
    own_count = lax.dynamic_slice_in_dim(kept_count, lax.axis_index(("z", "y")) * own_rows, own_rows)
    own_live = lax.broadcasted_iota(jnp.int32, (own_rows, MOSTR), 1) < own_count[:, None]
    block_grad = jnp.where(own_live[:, :, None], block_grad, jnp.float32(0.0))

    return (grads, block_grad)


def _split_mesh(mesh):
    devs = mesh.devices
    dp, seq = devs.shape
    ys = len({d.coords[1] for d in devs[:, 0]}) if hasattr(devs[0, 0], "coords") else 1
    cores = 2 if seq % 2 == 0 else 1
    return Mesh(devs.reshape(dp // ys, ys, seq // cores, cores), ("z", "y", "x", "c"))


def solution(mesh):
    fine = _split_mesh(mesh)
    rows = ("z", "y", "x", "c")
    placed = (
        P(rows, None),
        P(),
        P(rows, None),
        P(rows),
        P(),
        P(),
        P(("z", "y"), None, None),
    )
    return jax.shard_map(
        shards,
        mesh=fine,
        in_specs=placed,
        out_specs=(P(rows, None), P(("z", "y"), None, ("x", "c"))),
        check_vma=False,
    )
```

```python
import functools
import math

import jax
import jax.numpy as jnp
import numpy as np
from jax import lax
from jax.experimental import pallas as pl
from jax.experimental.pallas import tpu as pltpu
from jax.sharding import Mesh
from jax.sharding import PartitionSpec as P

D = 8192
KVW = 1024
HEAD_DIM = 128
BLK = 64
MOSTR = 6
SEQ_LEN = 1024
ROWS_PER_STEP = 32


def rope_back(grad, positions):
    heads = KVW // HEAD_DIM
    half = HEAD_DIM // 2
    values = grad.astype(jnp.float32).reshape(-1, heads, 2, half)
    freqs = 10000.0 ** (-2.0 * jnp.arange(half).astype(jnp.float32) / HEAD_DIM)
    angle = positions.astype(jnp.float32)[:, None] * freqs[None, :]
    cosine = jnp.cos(angle)[:, None, :]
    sine = jnp.sin(angle)[:, None, :]
    first = values[:, :, 0] * cosine + values[:, :, 1] * sine
    second = values[:, :, 1] * cosine - values[:, :, 0] * sine
    return jnp.stack([first, second], axis=2).reshape(-1, KVW).astype(jnp.bfloat16)


def _normed_grad_kernel(cols_ref, cnt_ref, gp_ref, bt_ref, out_ref, w_ref):
    step = pl.program_id(0)

    @pl.when(step == 0)
    def _():
        w_ref[...] = jnp.zeros(w_ref.shape, w_ref.dtype)

    def place(fill):
        for rr in range(ROWS_PER_STEP):
            row = step * ROWS_PER_STEP + rr
            live = cnt_ref[row]
            for k in range(MOSTR):
                start = pl.multiple_of(cols_ref[row * MOSTR + k] * BLK, BLK)
                if fill:
                    half = (k % 2) * BLK
                    value = bt_ref[rr, k // 2, :, half:half + BLK]
                    value = jnp.where(k < live, value, jnp.zeros_like(value))
                else:
                    value = jnp.zeros((BLK, BLK), w_ref.dtype)
                w_ref[pl.ds(start, BLK), rr * BLK:(rr + 1) * BLK] = value

    place(True)
    out_ref[...] = jnp.dot(gp_ref[...], w_ref[...], preferred_element_type=jnp.float32)
    place(False)


def normed_grad_of(grad_pre, blocks_t, cols, counts):
    tok = grad_pre.shape[0]
    row_blocks = blocks_t.shape[0]
    width = ROWS_PER_STEP * BLK
    spec = pltpu.PrefetchScalarGridSpec(
        num_scalar_prefetch=2,
        grid=(row_blocks // ROWS_PER_STEP,),
        in_specs=[
            pl.BlockSpec((tok, KVW), lambda g, c, n: (0, 0)),
            pl.BlockSpec((ROWS_PER_STEP, MOSTR // 2, BLK, 2 * BLK), lambda g, c, n: (g, 0, 0, 0)),
        ],
        out_specs=pl.BlockSpec((tok, width), lambda g, c, n: (0, g)),
        scratch_shapes=[pltpu.VMEM((KVW, width), jnp.bfloat16)],
    )
    return pl.pallas_call(
        _normed_grad_kernel,
        grid_spec=spec,
        out_shape=jax.ShapeDtypeStruct((tok, row_blocks * BLK), jnp.float32),
        compiler_params=pltpu.CompilerParams(dimension_semantics=("arbitrary",)),
    )(cols.reshape(-1), counts, grad_pre, blocks_t)


def _pick_kernel(cols_ref, cnt_ref, pt_ref, out_ref, *, part_rows, divisor):
    step = pl.program_id(0)
    width = pt_ref.shape[1]
    per_step = width // part_rows
    dests = out_ref.shape[0]
    sub = width // dests
    group = lax.broadcasted_iota(jnp.int32, (BLK, width), 1) // part_rows
    for k in range(MOSTR):
        acc = jnp.zeros((BLK, width), jnp.float32)
        for rr in range(per_step):
            row = step * per_step + rr
            start = pl.multiple_of(cols_ref[row * MOSTR + k] * BLK, BLK)
            acc = jnp.where(group == rr, pt_ref[pl.ds(start, BLK), :], acc)
        acc_t = (acc / divisor).T
        half = (k % 2) * BLK
        for d in range(dests):
            out_ref[d, k // 2, :, half:half + BLK] = acc_t[d * sub:(d + 1) * sub, :].astype(out_ref.dtype)


def pick_blocks(product_t, cols, counts, part_rows, divisor, devices):
    per_dev = product_t.shape[1] // devices
    width = max(256, per_dev)
    dests = width // per_dev
    chunks = product_t.shape[1] // width
    spec = pltpu.PrefetchScalarGridSpec(
        num_scalar_prefetch=2,
        grid=(chunks,),
        in_specs=[pl.BlockSpec((product_t.shape[0], width), lambda g, c, n: (0, g))],
        out_specs=pl.BlockSpec((dests, MOSTR // 2, per_dev, 2 * BLK), lambda g, c, n: (g, 0, 0, 0)),
    )
    return pl.pallas_call(
        functools.partial(_pick_kernel, part_rows=part_rows, divisor=divisor),
        grid_spec=spec,
        out_shape=jax.ShapeDtypeStruct((devices, MOSTR // 2, per_dev, 2 * BLK), jnp.bfloat16),
        compiler_params=pltpu.CompilerParams(dimension_semantics=("arbitrary",)),
    )(cols.reshape(-1), counts, product_t)


def shards(checkpoint, norm_gain, key_cotangent, positions, kept_cols, kept_count, key_blocks):
    tok_rows = checkpoint.shape[0]
    groups = lax.axis_size("x") * lax.axis_size("c")
    dp_size = lax.axis_size("z") * lax.axis_size("y")
    part_rows = BLK // groups
    row_blocks = D // BLK
    col_blocks = KVW // BLK
    xf = checkpoint.astype(jnp.float32)
    inv_rms = lax.rsqrt(jnp.mean(xf * xf, axis=1, keepdims=True) + 1e-05)
    normed = (xf * inv_rms * norm_gain).astype(jnp.bfloat16)
    grad_pre = rope_back(key_cotangent, positions)

    local_t = (
        key_blocks.reshape(key_blocks.shape[0], MOSTR // 2, 2, BLK, BLK)
        .transpose(0, 1, 4, 2, 3)
        .reshape(key_blocks.shape[0], MOSTR // 2, BLK, 2 * BLK)
    )
    piece = lax.all_gather(local_t, ("z", "y"), axis=0, tiled=True)

    split_normed = (
        normed.reshape(tok_rows, row_blocks, groups, part_rows)
        .transpose(0, 2, 1, 3)
        .reshape(tok_rows, groups, row_blocks * part_rows)
    )
    sent = jnp.concatenate(
        [split_normed, jnp.broadcast_to(grad_pre[:, None, :], (tok_rows, groups, KVW))], axis=2
    )
    received = lax.all_to_all(sent, ("x", "c"), split_axis=1, concat_axis=0, tiled=True)
    received = received.reshape(groups * tok_rows, row_blocks * part_rows + KVW)
    grad_all = received[:, row_blocks * part_rows:]
    normed_rows = received[:, : row_blocks * part_rows].reshape(groups * tok_rows, row_blocks, part_rows)
    divisor = math.sqrt(tok_rows * groups * dp_size)
    slab = normed_rows.reshape(groups * tok_rows, row_blocks * part_rows)
    product = lax.dot_general(
        grad_all, slab, (((0,), (0,)), ((), ())), preferred_element_type=jnp.float32
    )
    partial = pick_blocks(product, kept_cols, kept_count, part_rows, divisor, dp_size)
    partial, piece = lax.optimization_barrier((partial, piece))
    summed = lax.all_to_all(partial, ("z", "y"), split_axis=0, concat_axis=0, tiled=True)
    normed_grad = normed_grad_of(grad_pre, piece, kept_cols, kept_count)
    scaled = norm_gain * normed_grad
    grads = inv_rms * scaled - inv_rms**3 * xf * jnp.mean(scaled * xf, axis=1, keepdims=True)
    grads = grads.astype(jnp.bfloat16)
    summed, grads = lax.optimization_barrier((summed, grads))
    summed = summed.astype(jnp.float32).sum(axis=0)
    own_rows = summed.shape[1] // part_rows
    block_grad = (
        summed.reshape(MOSTR // 2, own_rows, part_rows, 2, BLK)
        .transpose(1, 0, 3, 2, 4)
        .reshape(own_rows, MOSTR, part_rows * BLK)
    )
    own_count = lax.dynamic_slice_in_dim(kept_count, lax.axis_index(("z", "y")) * own_rows, own_rows)
    own_live = lax.broadcasted_iota(jnp.int32, (own_rows, MOSTR), 1) < own_count[:, None]
    block_grad = jnp.where(own_live[:, :, None], block_grad, jnp.float32(0.0))

    return (grads, block_grad)


def _split_mesh(mesh):
    devs = mesh.devices
    dp, seq = devs.shape
    ys = len({d.coords[1] for d in devs[:, 0]}) if hasattr(devs[0, 0], "coords") else 1
    cores = 2 if seq % 2 == 0 else 1
    return Mesh(devs.reshape(dp // ys, ys, seq // cores, cores), ("z", "y", "x", "c"))


def solution(mesh):
    fine = _split_mesh(mesh)
    rows = ("z", "y", "x", "c")
    placed = (
        P(rows, None),
        P(),
        P(rows, None),
        P(rows),
        P(),
        P(),
        P(("z", "y"), None, None),
    )
    return jax.shard_map(
        shards,
        mesh=fine,
        in_specs=placed,
        out_specs=(P(rows, None), P(("z", "y"), None, ("x", "c"))),
        check_vma=False,
    )
```

```python
import functools
import math

import jax
import jax.numpy as jnp
import numpy as np
from jax import lax
from jax.experimental import pallas as pl
from jax.experimental.pallas import tpu as pltpu
from jax.sharding import Mesh
from jax.sharding import PartitionSpec as P

D = 8192
KVW = 1024
HEAD_DIM = 128
BLK = 64
MOSTR = 6
SEQ_LEN = 1024
ROWS_PER_STEP = 32


def rope_back(grad, positions):
    heads = KVW // HEAD_DIM
    half = HEAD_DIM // 2
    values = grad.astype(jnp.float32).reshape(-1, heads, 2, half)
    freqs = 10000.0 ** (-2.0 * jnp.arange(half).astype(jnp.float32) / HEAD_DIM)
    angle = positions.astype(jnp.float32)[:, None] * freqs[None, :]
    cosine = jnp.cos(angle)[:, None, :]
    sine = jnp.sin(angle)[:, None, :]
    first = values[:, :, 0] * cosine + values[:, :, 1] * sine
    second = values[:, :, 1] * cosine - values[:, :, 0] * sine
    return jnp.stack([first, second], axis=2).reshape(-1, KVW).astype(jnp.bfloat16)


def _normed_grad_kernel(cols_ref, cnt_ref, gp_ref, bt_ref, x_ref, gain_ref, out_ref, dot_ref, w_ref):
    step = pl.program_id(0)

    @pl.when(step == 0)
    def _():
        w_ref[...] = jnp.zeros(w_ref.shape, w_ref.dtype)
        dot_ref[...] = jnp.zeros(dot_ref.shape, dot_ref.dtype)

    def place(fill):
        for rr in range(ROWS_PER_STEP):
            row = step * ROWS_PER_STEP + rr
            live = cnt_ref[row]
            for k in range(MOSTR):
                start = pl.multiple_of(cols_ref[row * MOSTR + k] * BLK, BLK)
                if fill:
                    half = (k % 2) * BLK
                    value = bt_ref[rr, k // 2, :, half:half + BLK]
                    value = jnp.where(k < live, value, jnp.zeros_like(value))
                else:
                    value = jnp.zeros((BLK, BLK), w_ref.dtype)
                w_ref[pl.ds(start, BLK), rr * BLK:(rr + 1) * BLK] = value

    place(True)
    result = jnp.dot(gp_ref[...], w_ref[...], preferred_element_type=jnp.float32)
    out_ref[...] = result
    part = jnp.sum(gain_ref[...] * result * x_ref[...].astype(jnp.float32), axis=1, keepdims=True)
    dot_ref[...] += jnp.broadcast_to(part, dot_ref.shape)
    place(False)


def normed_grad_of(grad_pre, blocks_t, cols, counts, checkpoint, norm_gain):
    tok = grad_pre.shape[0]
    row_blocks = blocks_t.shape[0]
    width = ROWS_PER_STEP * BLK
    spec = pltpu.PrefetchScalarGridSpec(
        num_scalar_prefetch=2,
        grid=(row_blocks // ROWS_PER_STEP,),
        in_specs=[
            pl.BlockSpec((tok, KVW), lambda g, c, n: (0, 0)),
            pl.BlockSpec((ROWS_PER_STEP, MOSTR // 2, BLK, 2 * BLK), lambda g, c, n: (g, 0, 0, 0)),
            pl.BlockSpec((tok, width), lambda g, c, n: (0, g)),
            pl.BlockSpec((1, width), lambda g, c, n: (0, g)),
        ],
        out_specs=[
            pl.BlockSpec((tok, width), lambda g, c, n: (0, g)),
            pl.BlockSpec((tok, 128), lambda g, c, n: (0, 0)),
        ],
        scratch_shapes=[pltpu.VMEM((KVW, width), jnp.bfloat16)],
    )
    return pl.pallas_call(
        _normed_grad_kernel,
        grid_spec=spec,
        out_shape=(
            jax.ShapeDtypeStruct((tok, row_blocks * BLK), jnp.float32),
            jax.ShapeDtypeStruct((tok, 128), jnp.float32),
        ),
        compiler_params=pltpu.CompilerParams(dimension_semantics=("arbitrary",)),
    )(cols.reshape(-1), counts, grad_pre, blocks_t, checkpoint, norm_gain.reshape(1, -1))


def _pick_kernel(cols_ref, cnt_ref, pt_ref, out_ref, *, part_rows, divisor):
    step = pl.program_id(0)
    width = pt_ref.shape[1]
    per_step = width // part_rows
    dests = out_ref.shape[0]
    sub = width // dests
    group = lax.broadcasted_iota(jnp.int32, (BLK, width), 1) // part_rows
    for k in range(MOSTR):
        acc = jnp.zeros((BLK, width), jnp.float32)
        for rr in range(per_step):
            row = step * per_step + rr
            start = pl.multiple_of(cols_ref[row * MOSTR + k] * BLK, BLK)
            acc = jnp.where(group == rr, pt_ref[pl.ds(start, BLK), :], acc)
        acc_t = (acc / divisor).T
        half = (k % 2) * BLK
        for d in range(dests):
            out_ref[d, k // 2, :, half:half + BLK] = acc_t[d * sub:(d + 1) * sub, :].astype(out_ref.dtype)


def pick_blocks(product_t, cols, counts, part_rows, divisor, devices):
    per_dev = product_t.shape[1] // devices
    width = max(256, per_dev)
    dests = width // per_dev
    chunks = product_t.shape[1] // width
    spec = pltpu.PrefetchScalarGridSpec(
        num_scalar_prefetch=2,
        grid=(chunks,),
        in_specs=[pl.BlockSpec((product_t.shape[0], width), lambda g, c, n: (0, g))],
        out_specs=pl.BlockSpec((dests, MOSTR // 2, per_dev, 2 * BLK), lambda g, c, n: (g, 0, 0, 0)),
    )
    return pl.pallas_call(
        functools.partial(_pick_kernel, part_rows=part_rows, divisor=divisor),
        grid_spec=spec,
        out_shape=jax.ShapeDtypeStruct((devices, MOSTR // 2, per_dev, 2 * BLK), jnp.bfloat16),
        compiler_params=pltpu.CompilerParams(dimension_semantics=("arbitrary",)),
    )(cols.reshape(-1), counts, product_t)


def shards(checkpoint, norm_gain, key_cotangent, positions, kept_cols, kept_count, key_blocks):
    tok_rows = checkpoint.shape[0]
    groups = lax.axis_size("x") * lax.axis_size("c")
    dp_size = lax.axis_size("z") * lax.axis_size("y")
    part_rows = BLK // groups
    row_blocks = D // BLK
    col_blocks = KVW // BLK
    xf = checkpoint.astype(jnp.float32)
    inv_rms = lax.rsqrt(jnp.mean(xf * xf, axis=1, keepdims=True) + 1e-05)
    normed = (xf * inv_rms * norm_gain).astype(jnp.bfloat16)
    grad_pre = rope_back(key_cotangent, positions)

    local_t = (
        key_blocks.reshape(key_blocks.shape[0], MOSTR // 2, 2, BLK, BLK)
        .transpose(0, 1, 4, 2, 3)
        .reshape(key_blocks.shape[0], MOSTR // 2, BLK, 2 * BLK)
    )
    piece = lax.all_gather(local_t, ("z", "y"), axis=0, tiled=True)

    split_normed = (
        normed.reshape(tok_rows, row_blocks, groups, part_rows)
        .transpose(0, 2, 1, 3)
        .reshape(tok_rows, groups, row_blocks * part_rows)
    )
    sent = jnp.concatenate(
        [split_normed, jnp.broadcast_to(grad_pre[:, None, :], (tok_rows, groups, KVW))], axis=2
    )
    received = lax.all_to_all(sent, ("x", "c"), split_axis=1, concat_axis=0, tiled=True)
    received = received.reshape(groups * tok_rows, row_blocks * part_rows + KVW)
    grad_all = received[:, row_blocks * part_rows:]
    normed_rows = received[:, : row_blocks * part_rows].reshape(groups * tok_rows, row_blocks, part_rows)
    divisor = math.sqrt(tok_rows * groups * dp_size)
    slab = normed_rows.reshape(groups * tok_rows, row_blocks * part_rows)
    product = lax.dot_general(
        grad_all, slab, (((0,), (0,)), ((), ())), preferred_element_type=jnp.float32
    )
    partial = pick_blocks(product, kept_cols, kept_count, part_rows, divisor, dp_size)
    partial, piece = lax.optimization_barrier((partial, piece))
    summed = lax.all_to_all(partial, ("z", "y"), split_axis=0, concat_axis=0, tiled=True)
    normed_grad, row_dot = normed_grad_of(grad_pre, piece, kept_cols, kept_count, checkpoint, norm_gain)
    scaled = norm_gain * normed_grad
    grads = inv_rms * scaled - inv_rms**3 * xf * (row_dot[:, :1] / D)
    grads = grads.astype(jnp.bfloat16)
    summed, grads = lax.optimization_barrier((summed, grads))
    summed = summed.astype(jnp.float32).sum(axis=0)
    own_rows = summed.shape[1] // part_rows
    block_grad = (
        summed.reshape(MOSTR // 2, own_rows, part_rows, 2, BLK)
        .transpose(1, 0, 3, 2, 4)
        .reshape(own_rows, MOSTR, part_rows * BLK)
    )
    own_count = lax.dynamic_slice_in_dim(kept_count, lax.axis_index(("z", "y")) * own_rows, own_rows)
    own_live = lax.broadcasted_iota(jnp.int32, (own_rows, MOSTR), 1) < own_count[:, None]
    block_grad = jnp.where(own_live[:, :, None], block_grad, jnp.float32(0.0))

    return (grads, block_grad)


def _split_mesh(mesh):
    devs = mesh.devices
    dp, seq = devs.shape
    ys = len({d.coords[1] for d in devs[:, 0]}) if hasattr(devs[0, 0], "coords") else 1
    cores = 2 if seq % 2 == 0 else 1
    return Mesh(devs.reshape(dp // ys, ys, seq // cores, cores), ("z", "y", "x", "c"))


def solution(mesh):
    fine = _split_mesh(mesh)
    rows = ("z", "y", "x", "c")
    placed = (
        P(rows, None),
        P(),
        P(rows, None),
        P(rows),
        P(),
        P(),
        P(("z", "y"), None, None),
    )
    return jax.shard_map(
        shards,
        mesh=fine,
        in_specs=placed,
        out_specs=(P(rows, None), P(("z", "y"), None, ("x", "c"))),
        check_vma=False,
    )
```

```python
import functools
import math

import jax
import jax.numpy as jnp
import numpy as np
from jax import lax
from jax.experimental import pallas as pl
from jax.experimental.pallas import tpu as pltpu
from jax.sharding import Mesh
from jax.sharding import PartitionSpec as P

D = 8192
KVW = 1024
HEAD_DIM = 128
BLK = 64
MOSTR = 6
SEQ_LEN = 1024
ROWS_PER_STEP = 64


def rope_back(grad, positions):
    heads = KVW // HEAD_DIM
    half = HEAD_DIM // 2
    values = grad.astype(jnp.float32).reshape(-1, heads, 2, half)
    freqs = 10000.0 ** (-2.0 * jnp.arange(half).astype(jnp.float32) / HEAD_DIM)
    angle = positions.astype(jnp.float32)[:, None] * freqs[None, :]
    cosine = jnp.cos(angle)[:, None, :]
    sine = jnp.sin(angle)[:, None, :]
    first = values[:, :, 0] * cosine + values[:, :, 1] * sine
    second = values[:, :, 1] * cosine - values[:, :, 0] * sine
    return jnp.stack([first, second], axis=2).reshape(-1, KVW).astype(jnp.bfloat16)


def _normed_grad_kernel(cols_ref, cnt_ref, gp_ref, bt_ref, out_ref, w_ref):
    step = pl.program_id(0)

    @pl.when(step == 0)
    def _():
        w_ref[...] = jnp.zeros(w_ref.shape, w_ref.dtype)

    def place(fill):
        for rr in range(ROWS_PER_STEP):
            row = step * ROWS_PER_STEP + rr
            live = cnt_ref[row]
            for k in range(MOSTR):
                start = pl.multiple_of(cols_ref[row * MOSTR + k] * BLK, BLK)
                if fill:
                    half = (k % 2) * BLK
                    value = bt_ref[rr, k // 2, :, half:half + BLK]
                    value = jnp.where(k < live, value, jnp.zeros_like(value))
                else:
                    value = jnp.zeros((BLK, BLK), w_ref.dtype)
                w_ref[pl.ds(start, BLK), rr * BLK:(rr + 1) * BLK] = value

    place(True)
    out_ref[...] = jnp.dot(gp_ref[...], w_ref[...], preferred_element_type=jnp.float32)
    place(False)


def normed_grad_of(grad_pre, blocks_t, cols, counts):
    tok = grad_pre.shape[0]
    row_blocks = blocks_t.shape[0]
    width = ROWS_PER_STEP * BLK
    spec = pltpu.PrefetchScalarGridSpec(
        num_scalar_prefetch=2,
        grid=(row_blocks // ROWS_PER_STEP,),
        in_specs=[
            pl.BlockSpec((tok, KVW), lambda g, c, n: (0, 0)),
            pl.BlockSpec((ROWS_PER_STEP, MOSTR // 2, BLK, 2 * BLK), lambda g, c, n: (g, 0, 0, 0)),
        ],
        out_specs=pl.BlockSpec((tok, width), lambda g, c, n: (0, g)),
        scratch_shapes=[pltpu.VMEM((KVW, width), jnp.bfloat16)],
    )
    return pl.pallas_call(
        _normed_grad_kernel,
        grid_spec=spec,
        out_shape=jax.ShapeDtypeStruct((tok, row_blocks * BLK), jnp.float32),
        compiler_params=pltpu.CompilerParams(dimension_semantics=("arbitrary",)),
    )(cols.reshape(-1), counts, grad_pre, blocks_t)


def _pick_kernel(cols_ref, cnt_ref, pt_ref, out_ref, *, part_rows, divisor):
    step = pl.program_id(0)
    width = pt_ref.shape[1]
    per_step = width // part_rows
    dests = out_ref.shape[0]
    sub = width // dests
    group = lax.broadcasted_iota(jnp.int32, (BLK, width), 1) // part_rows
    for k in range(MOSTR):
        acc = jnp.zeros((BLK, width), jnp.float32)
        for rr in range(per_step):
            row = step * per_step + rr
            start = pl.multiple_of(cols_ref[row * MOSTR + k] * BLK, BLK)
            acc = jnp.where(group == rr, pt_ref[pl.ds(start, BLK), :], acc)
        acc_t = (acc / divisor).T
        half = (k % 2) * BLK
        for d in range(dests):
            out_ref[d, k // 2, :, half:half + BLK] = acc_t[d * sub:(d + 1) * sub, :].astype(out_ref.dtype)


def pick_blocks(product_t, cols, counts, part_rows, divisor, devices):
    per_dev = product_t.shape[1] // devices
    width = max(512, per_dev)
    dests = width // per_dev
    chunks = product_t.shape[1] // width
    spec = pltpu.PrefetchScalarGridSpec(
        num_scalar_prefetch=2,
        grid=(chunks,),
        in_specs=[pl.BlockSpec((product_t.shape[0], width), lambda g, c, n: (0, g))],
        out_specs=pl.BlockSpec((dests, MOSTR // 2, per_dev, 2 * BLK), lambda g, c, n: (g, 0, 0, 0)),
    )
    return pl.pallas_call(
        functools.partial(_pick_kernel, part_rows=part_rows, divisor=divisor),
        grid_spec=spec,
        out_shape=jax.ShapeDtypeStruct((devices, MOSTR // 2, per_dev, 2 * BLK), jnp.bfloat16),
        compiler_params=pltpu.CompilerParams(dimension_semantics=("arbitrary",)),
    )(cols.reshape(-1), counts, product_t)


def shards(checkpoint, norm_gain, key_cotangent, positions, kept_cols, kept_count, key_blocks):
    tok_rows = checkpoint.shape[0]
    groups = lax.axis_size("x") * lax.axis_size("c")
    dp_size = lax.axis_size("z") * lax.axis_size("y")
    part_rows = BLK // groups
    row_blocks = D // BLK
    col_blocks = KVW // BLK
    xf = checkpoint.astype(jnp.float32)
    inv_rms = lax.rsqrt(jnp.mean(xf * xf, axis=1, keepdims=True) + 1e-05)
    normed = (xf * inv_rms * norm_gain).astype(jnp.bfloat16)
    grad_pre = rope_back(key_cotangent, positions)

    local_t = (
        key_blocks.reshape(key_blocks.shape[0], MOSTR // 2, 2, BLK, BLK)
        .transpose(0, 1, 4, 2, 3)
        .reshape(key_blocks.shape[0], MOSTR // 2, BLK, 2 * BLK)
    )
    piece = lax.all_gather(local_t, ("z", "y"), axis=0, tiled=True)

    split_normed = (
        normed.reshape(tok_rows, row_blocks, groups, part_rows)
        .transpose(0, 2, 1, 3)
        .reshape(tok_rows, groups, row_blocks * part_rows)
    )
    sent = jnp.concatenate(
        [split_normed, jnp.broadcast_to(grad_pre[:, None, :], (tok_rows, groups, KVW))], axis=2
    )
    received = lax.all_to_all(sent, ("x", "c"), split_axis=1, concat_axis=0, tiled=True)
    received = received.reshape(groups * tok_rows, row_blocks * part_rows + KVW)
    grad_all = received[:, row_blocks * part_rows:]
    normed_rows = received[:, : row_blocks * part_rows].reshape(groups * tok_rows, row_blocks, part_rows)
    divisor = math.sqrt(tok_rows * groups * dp_size)
    slab = normed_rows.reshape(groups * tok_rows, row_blocks * part_rows)
    product = lax.dot_general(
        grad_all, slab, (((0,), (0,)), ((), ())), preferred_element_type=jnp.float32
    )
    partial = pick_blocks(product, kept_cols, kept_count, part_rows, divisor, dp_size)
    partial, piece = lax.optimization_barrier((partial, piece))
    summed = lax.all_to_all(partial, ("z", "y"), split_axis=0, concat_axis=0, tiled=True)
    normed_grad = normed_grad_of(grad_pre, piece, kept_cols, kept_count)
    scaled = norm_gain * normed_grad
    grads = inv_rms * scaled - inv_rms**3 * xf * jnp.mean(scaled * xf, axis=1, keepdims=True)
    grads = grads.astype(jnp.bfloat16)
    summed, grads = lax.optimization_barrier((summed, grads))
    summed = summed.astype(jnp.float32).sum(axis=0)
    own_rows = summed.shape[1] // part_rows
    block_grad = (
        summed.reshape(MOSTR // 2, own_rows, part_rows, 2, BLK)
        .transpose(1, 0, 3, 2, 4)
        .reshape(own_rows, MOSTR, part_rows * BLK)
    )
    own_count = lax.dynamic_slice_in_dim(kept_count, lax.axis_index(("z", "y")) * own_rows, own_rows)
    own_live = lax.broadcasted_iota(jnp.int32, (own_rows, MOSTR), 1) < own_count[:, None]
    block_grad = jnp.where(own_live[:, :, None], block_grad, jnp.float32(0.0))

    return (grads, block_grad)


def _split_mesh(mesh):
    devs = mesh.devices
    dp, seq = devs.shape
    ys = len({d.coords[1] for d in devs[:, 0]}) if hasattr(devs[0, 0], "coords") else 1
    cores = 2 if seq % 2 == 0 else 1
    return Mesh(devs.reshape(dp // ys, ys, seq // cores, cores), ("z", "y", "x", "c"))


def solution(mesh):
    fine = _split_mesh(mesh)
    rows = ("z", "y", "x", "c")
    placed = (
        P(rows, None),
        P(),
        P(rows, None),
        P(rows),
        P(),
        P(),
        P(("z", "y"), None, None),
    )
    return jax.shard_map(
        shards,
        mesh=fine,
        in_specs=placed,
        out_specs=(P(rows, None), P(("z", "y"), None, ("x", "c"))),
        check_vma=False,
    )
```
